256 devices in a mesh: sample: 8 (over z_lo, y), space: 32 (over x, z_hi, core).
Axes of the slice: x: 4, y: 4, z: 8 (z_hi: 4, z_lo: 2; z = z_hi * 2 + z_lo), core: 2. Of those that a mesh axis runs over, the one named last changes fastest.
Arguments:
- volume: bfloat16 [64, 8, 32, 1024], P('space', 'sample'), may hold values from -6 to 6
- out_grads: bfloat16 [32, 8, 128, 256], P('space', 'sample'), may hold values from -6 to 6
- kernel_one: bfloat16 [27, 32, 64], replicated, may hold values from -0.21875 to 0.21875
- kernel_two: bfloat16 [27, 64, 128], replicated, may hold values from -0.15625 to 0.15625
Outputs:
- layer_out: bfloat16 [32, 8, 128, 256], P('space', 'sample')
- input_grads: bfloat16 [64, 8, 32, 1024], P('space', 'sample')
- kernel_one_grads: float32 [27, 32, 64], replicated
- kernel_two_grads: float32 [27, 64, 128], replicated
The draws below stay inside these ranges and needn't reach their ends.
All inputs are finite; a program needn't handle non-finite values.
Results may differ from the reference program's by a relative error of at most 0.015.
Values may be sent and summed in bfloat16 or wider, within the bound.
No kernel may reach another device: no remote copies, remote signals or barrier semaphores. Data moves between devices by JAX's collectives and lax.ppermute only.
A program may use at most 128 MiB of HBM per device.

```python
import jax
import jax.numpy as jnp
from jax import lax

CIN = 32
C1 = 64
C2 = 128
SIDE = 32
Z = 64
BATCH = 8
PLANE = 1024
HALF = 16
Z2 = 32
PLANE2 = 256


def steps_of(stream_key, dims, shards, smallest, largest):
    def one(dim, shards_of):
        steps = jax.random.uniform(jax.random.fold_in(jax.random.fold_in(stream_key, 6), dim), (shards_of,), jnp.float32, smallest / len(shards), largest / len(shards))
        return jnp.repeat(jnp.exp(steps), dims[dim] // shards_of).reshape((-1,) + (1,) * (len(dims) - dim - 1))

    level = one(*shards[0])
    for cut in shards[1:]:
        level = level * one(*cut)
    return level


def bell_draw(key, extent, width, reach, shards=(), held_as=jnp.bfloat16):
    drawn = jax.random.normal(key, extent, jnp.float32) * width
    if len(shards) > 0:
        drawn = steps_of(key, extent, shards, -0.22, 0.18) * drawn
    return jnp.clip(drawn, min=-reach, max=reach).astype(held_as)


def setup_inputs(seed: int = 0) -> dict:
    splits = jax.random.split(jax.random.key(seed), 5)
    volume = bell_draw(splits[0], (Z, BATCH, CIN, PLANE), 1.0, 6.0, ((0, 32), (1, 8)))
    out_grads = bell_draw(splits[1], (Z2, BATCH, C2, PLANE2), 1.0, 6.0, ((0, 32), (1, 8)))
    kernel_one = bell_draw(splits[2], (27, CIN, C1), (27 * CIN) ** -0.5, 0.21875)
    kernel_two = bell_draw(splits[3], (27, C1, C2), (27 * C1) ** -0.5, 0.15625)
    return dict(volume=volume, out_grads=out_grads, kernel_one=kernel_one, kernel_two=kernel_two)


def convolve(inputs, kernel, stride):
    cube = kernel.reshape(3, 3, 3, kernel.shape[1], kernel.shape[2])
    return lax.conv_general_dilated(inputs, cube, (stride, stride, stride), [(1, 1), (1, 1), (1, 1)], dimension_numbers=('DNCHW', 'DHWIO', 'DNCHW'), precision=lax.Precision.HIGHEST)

def reference(volume, out_grads, kernel_one, kernel_two):
    cells = volume.astype(jnp.float32).reshape(Z, BATCH, CIN, SIDE, SIDE)
    first = kernel_one.astype(jnp.float32)
    second = kernel_two.astype(jnp.float32)
    pre_one, pull_one = jax.vjp(lambda inputs, kernel: convolve(inputs, kernel, 1), cells, first)
    hidden = lax.optimization_barrier(jax.nn.silu(pre_one).astype(jnp.bfloat16)).astype(jnp.float32)
    strided, pull_two = jax.vjp(lambda inputs, kernel: convolve(inputs, kernel, 2), hidden, second)
    layer_out = strided.astype(jnp.bfloat16).reshape(Z2, BATCH, C2, PLANE2)
    cotangent = out_grads.astype(jnp.float32).reshape(Z2, BATCH, C2, HALF, HALF)
    hidden_grads, kernel_two_grads = pull_two(cotangent)
    hidden_grads = lax.optimization_barrier(hidden_grads.astype(jnp.bfloat16)).astype(jnp.float32)
    sigma = jax.nn.sigmoid(pre_one)
    pre_grads = hidden_grads * sigma * (1.0 + pre_one * (1.0 - sigma))
    pre_grads = lax.optimization_barrier(pre_grads.astype(jnp.bfloat16)).astype(jnp.float32)
    input_grads, kernel_one_grads = pull_one(pre_grads)
    input_grads = input_grads.astype(jnp.bfloat16).reshape(Z, BATCH, CIN, PLANE)
    kernel_one_grads = kernel_one_grads * float(BATCH * Z * PLANE) ** (-0.5)
    kernel_two_grads = kernel_two_grads * float(BATCH * Z2 * PLANE2) ** (-0.5)
    return (layer_out, input_grads, kernel_one_grads, kernel_two_grads)
```

```python
import jax
import jax.numpy as jnp
from jax import lax
from jax.sharding import PartitionSpec as P

SIDE = 32


def with_halo(block, sides, width):
    for axis, dim in sides:
        count = lax.axis_size(axis)
        forward = [(i, i + 1) for i in range(count - 1)]
        backward = [(target, source) for source, target in forward]
        low = lax.ppermute(
            lax.slice_in_dim(block, block.shape[dim] - width, None, axis=dim), axis, forward
        )
        high = lax.ppermute(lax.slice_in_dim(block, 0, width, axis=dim), axis, backward)
        block = jnp.concatenate([low, block, high], axis=dim)
    return block


def passed_along(block, axis, distance):
    devices = range(lax.axis_size(axis))
    route = [(i - distance, i) for i in devices if i - distance in devices]
    return lax.ppermute(block, axis, route)


def convolve(inputs, kernel, stride, margins, dilation):
    return lax.conv_general_dilated(
        inputs,
        kernel,
        (stride, stride, stride),
        margins,
        lhs_dilation=(dilation, dilation, dilation),
        dimension_numbers=("DNCHW", "DHWIO", "DNCHW"),
        preferred_element_type=jnp.float32,
    )


def kernel_cube(kernel):
    return kernel.reshape(3, 3, 3, kernel.shape[1], kernel.shape[2])


def reversed_kernel(kernel):
    cube = kernel_cube(kernel)
    return jnp.transpose(cube[::-1, ::-1, ::-1], (0, 1, 2, 4, 3))


def weight_grad(padded, grads, stride):
    depth_out, rows_out, cols_out = (grads.shape[0], grads.shape[3], grads.shape[4])
    if stride == 1:
        phases = padded[None, None]
    else:
        depth, batch, channels, rows, cols = padded.shape
        phases = padded.reshape(depth, batch, channels, rows // 2, 2, cols // 2, 2)
        phases = jnp.transpose(phases, (4, 6, 0, 1, 2, 3, 5))
    windows = []
    for depth_tap in range(3):
        for row_tap in range(3):
            for col_tap in range(3):
                phase = phases[row_tap % stride, col_tap % stride]
                row0, col0 = row_tap // stride, col_tap // stride
                windows.append(
                    lax.slice(
                        phase,
                        (depth_tap, 0, 0, row0, col0),
                        (
                            depth_tap + stride * (depth_out - 1) + 1,
                            phase.shape[1],
                            phase.shape[2],
                            row0 + rows_out,
                            col0 + cols_out,
                        ),
                        (stride, 1, 1, 1, 1),
                    )
                )
    return jnp.einsum(
        "tzbiyx,zboyx->tio", jnp.stack(windows), grads, preferred_element_type=jnp.float32
    )


HALVING_STEPS = (
    ("space", 1),
    ("sample", 1),
    ("sample", 4),
    ("space", 8),
    ("sample", 2),
    ("space", 16),
    ("space", 2),
    ("space", 4),
)


def all_sum(parts):
    flat = jnp.concatenate([part.reshape(-1) for part in parts])
    steps = []
    for axis, distance in HALVING_STEPS:
        if distance < lax.axis_size(axis):
            steps.append((axis, distance))
    count = 1
    for axis, _ in steps:
        count *= 2
    total = flat.shape[0]
    padded_total = -(-total // count) * count
    value = jnp.pad(flat, (0, padded_total - total))
    for axis, distance in steps:
        pairs = [(i, i ^ distance) for i in range(lax.axis_size(axis))]
        upper = (lax.axis_index(axis) // distance) % 2 == 1
        half = value.shape[0] // 2
        low, high = value[:half], value[half:]
        sent = jnp.where(upper, low, high)
        kept = jnp.where(upper, high, low)
        value = kept + lax.ppermute(sent, axis, pairs)
    for axis, distance in reversed(steps):
        pairs = [(i, i ^ distance) for i in range(lax.axis_size(axis))]
        upper = (lax.axis_index(axis) // distance) % 2 == 1
        other = lax.ppermute(value, axis, pairs)
        value = jnp.where(
            upper, jnp.concatenate([other, value]), jnp.concatenate([value, other])
        )
    results = []
    offset = 0
    for part in parts:
        results.append(value[offset : offset + part.size].reshape(part.shape))
        offset += part.size
    return results


def local(volume, out_grads, kernel_one, kernel_two):
    depth, batch, channels_in, plane = volume.shape
    channels_two = kernel_two.shape[2]
    half_side = SIDE // 2
    space_count = lax.axis_size("space")
    sample_count = lax.axis_size("sample")
    scale_one = float(sample_count * batch * space_count * depth * plane) ** (-0.5)
    scale_two = scale_one * 8.0**0.5
    cells = volume.reshape(depth, batch, channels_in, SIDE, SIDE)
    grads_cells = out_grads.reshape(depth // 2, batch, channels_two, half_side, half_side)
    framed = with_halo(cells, (("space", 0),), 1)
    pre_one = convolve(framed, kernel_cube(kernel_one), 1, [(0, 0), (1, 1), (1, 1)], 1)
    hidden = jax.nn.silu(pre_one).astype(jnp.bfloat16)
    below = passed_along(hidden[-1:], "space", 1)
    stacked = jnp.pad(jnp.concatenate([below, hidden], 0), ((0, 0), (0, 0), (0, 0), (1, 1), (1, 1)))
    strided = convolve(stacked, kernel_cube(kernel_two), 2, [(0, 0), (0, 0), (0, 0)], 1)
    above = passed_along(grads_cells, "space", -1)
    spread = convolve(
        jnp.concatenate([grads_cells, above], 0),
        reversed_kernel(kernel_two),
        1,
        [(1, 0), (1, 2), (1, 2)],
        2,
    )
    hidden_grads = spread.astype(jnp.bfloat16)
    local_two = weight_grad(stacked, grads_cells, 2) * scale_two
    layer_out = strided.astype(jnp.bfloat16).reshape(depth // 2, batch, channels_two, plane // 4)
    sigma = jax.nn.sigmoid(pre_one)
    pre_grads = (hidden_grads.astype(jnp.float32) * sigma * (1.0 + pre_one * (1.0 - sigma))).astype(
        jnp.bfloat16
    )
    framed_grads = with_halo(pre_grads, (("space", 0),), 1)
    input_grads = convolve(
        framed_grads, reversed_kernel(kernel_one), 1, [(0, 0), (1, 1), (1, 1)], 1
    ).astype(jnp.bfloat16)
    padded_input = jnp.pad(framed, ((0, 0), (0, 0), (0, 0), (1, 1), (1, 1)))
    first_grads = weight_grad(padded_input, pre_grads, 1) * scale_one
    first_grads, second_grads = all_sum([first_grads, local_two])
    return (
        layer_out,
        input_grads.reshape(depth, batch, channels_in, plane),
        first_grads,
        second_grads,
    )


def solution(mesh):
    in_specs = (P("space", "sample", None, None), P("space", "sample", None, None), P(), P())
    out_specs = (P("space", "sample", None, None), P("space", "sample", None, None), P(), P())
    return jax.shard_map(local, mesh=mesh, in_specs=in_specs, out_specs=out_specs, check_vma=False)
```

```python
import jax
import jax.numpy as jnp
from jax import lax
from jax.sharding import PartitionSpec as P

SIDE = 32


def with_halo(block, sides, width):
    for axis, dim in sides:
        count = lax.axis_size(axis)
        forward = [(i, i + 1) for i in range(count - 1)]
        backward = [(target, source) for source, target in forward]
        low = lax.ppermute(
            lax.slice_in_dim(block, block.shape[dim] - width, None, axis=dim), axis, forward
        )
        high = lax.ppermute(lax.slice_in_dim(block, 0, width, axis=dim), axis, backward)
        block = jnp.concatenate([low, block, high], axis=dim)
    return block


def passed_along(block, axis, distance):
    devices = range(lax.axis_size(axis))
    route = [(i - distance, i) for i in devices if i - distance in devices]
    return lax.ppermute(block, axis, route)


def convolve(inputs, kernel, stride, margins, dilation):
    return lax.conv_general_dilated(
        inputs,
        kernel,
        (stride, stride, stride),
        margins,
        lhs_dilation=(dilation, dilation, dilation),
        dimension_numbers=("DNCHW", "DHWIO", "DNCHW"),
        preferred_element_type=jnp.float32,
    )


def kernel_cube(kernel):
    return kernel.reshape(3, 3, 3, kernel.shape[1], kernel.shape[2])


def reversed_kernel(kernel):
    cube = kernel_cube(kernel)
    return jnp.transpose(cube[::-1, ::-1, ::-1], (0, 1, 2, 4, 3))


def weight_grad(padded, grads, stride):
    depth_out, rows_out, cols_out = (grads.shape[0], grads.shape[3], grads.shape[4])
    if stride == 1:
        phases = padded[None, None]
    else:
        depth, batch, channels, rows, cols = padded.shape
        phases = padded.reshape(depth, batch, channels, rows // 2, 2, cols // 2, 2)
        phases = jnp.transpose(phases, (4, 6, 0, 1, 2, 3, 5))
    windows = []
    for depth_tap in range(3):
        for row_tap in range(3):
            for col_tap in range(3):
                phase = phases[row_tap % stride, col_tap % stride]
                row0, col0 = row_tap // stride, col_tap // stride
                windows.append(
                    lax.slice(
                        phase,
                        (depth_tap, 0, 0, row0, col0),
                        (
                            depth_tap + stride * (depth_out - 1) + 1,
                            phase.shape[1],
                            phase.shape[2],
                            row0 + rows_out,
                            col0 + cols_out,
                        ),
                        (stride, 1, 1, 1, 1),
                    )
                )
    return jnp.einsum(
        "tzbiyx,zboyx->tio", jnp.stack(windows), grads, preferred_element_type=jnp.float32
    )


ROUNDS = (
    ("space", 1, 2),
    ("sample", 1, 4),
    ("sample", 4, 2),
    ("space", 8, 4),
    ("space", 2, 4),
)


def group_pairs(count, stride, radix, shift):
    pairs = []
    for i in range(count):
        g = (i // stride) % radix
        pairs.append((i, i + (((g + shift) % radix) - g) * stride))
    return pairs


def all_sum(parts):
    flat = jnp.concatenate([part.reshape(-1) for part in parts])
    rounds = []
    count = 1
    for axis, stride, radix in ROUNDS:
        if stride * radix <= lax.axis_size(axis):
            rounds.append((axis, stride, radix))
            count *= radix
    total = flat.shape[0]
    value = jnp.pad(flat, (0, -(-total // count) * count - total))
    for axis, stride, radix in rounds:
        size = lax.axis_size(axis)
        g = (lax.axis_index(axis) // stride) % radix
        chunks = value.reshape(radix, -1)
        value = lax.dynamic_index_in_dim(chunks, g, 0, keepdims=False)
        for shift in range(1, radix):
            sent = lax.dynamic_index_in_dim(chunks, (g + shift) % radix, 0, keepdims=False)
            value = value + lax.ppermute(sent, axis, group_pairs(size, stride, radix, shift))
    for axis, stride, radix in reversed(rounds):
        size = lax.axis_size(axis)
        g = (lax.axis_index(axis) // stride) % radix
        got = {
            shift: lax.ppermute(value, axis, group_pairs(size, stride, radix, shift))
            for shift in range(1, radix)
        }
        rolled = jnp.concatenate([value] + [got[radix - k] for k in range(1, radix)])
        value = jnp.roll(rolled, g * value.shape[0])
    results = []
    offset = 0
    for part in parts:
        results.append(value[offset : offset + part.size].reshape(part.shape))
        offset += part.size
    return results


def first_weight_grad(framed, grads):
    depth, batch, channels, side, _ = framed.shape
    depth_out = grads.shape[0]
    plane = side * side
    cells = jnp.transpose(framed.reshape(depth, batch, channels, plane), (2, 1, 0, 3))
    cells = jnp.pad(cells, ((0, 0), (0, 0), (0, 0), (side + 1, side + 1)))
    flat_grads = jnp.transpose(grads.reshape(depth_out, batch, -1, plane), (2, 1, 0, 3))
    column = lax.broadcasted_iota(jnp.int32, (1, 1, 1, plane), 3) % side
    per_column = []
    for col_tap in range(3):
        if col_tap == 0:
            masked = jnp.where(column == 0, 0, flat_grads)
        elif col_tap == 2:
            masked = jnp.where(column == side - 1, 0, flat_grads)
        else:
            masked = flat_grads
        windows = []
        for depth_tap in range(3):
            for row_tap in range(3):
                start = (side + 1) + (row_tap - 1) * side + (col_tap - 1)
                windows.append(
                    lax.slice(
                        cells,
                        (0, 0, depth_tap, start),
                        (channels, batch, depth_tap + depth_out, start + plane),
                    )
                )
        per_column.append(
            jnp.einsum(
                "tibzs,obzs->tio",
                jnp.stack(windows),
                masked.astype(cells.dtype),
                preferred_element_type=jnp.float32,
            )
        )
    stacked = jnp.stack(per_column, 1)
    return stacked.reshape(27, channels, -1)


def local(volume, out_grads, kernel_one, kernel_two):
    depth, batch, channels_in, plane = volume.shape
    channels_two = kernel_two.shape[2]
    half_side = SIDE // 2
    space_count = lax.axis_size("space")
    sample_count = lax.axis_size("sample")
    scale_one = float(sample_count * batch * space_count * depth * plane) ** (-0.5)
    scale_two = scale_one * 8.0**0.5
    cells = volume.reshape(depth, batch, channels_in, SIDE, SIDE)
    grads_cells = out_grads.reshape(depth // 2, batch, channels_two, half_side, half_side)
    framed = with_halo(cells, (("space", 0),), 1)
    pre_one = convolve(framed, kernel_cube(kernel_one), 1, [(0, 0), (1, 1), (1, 1)], 1)
    hidden = jax.nn.silu(pre_one).astype(jnp.bfloat16)
    below = passed_along(hidden[-1:], "space", 1)
    stacked = jnp.pad(jnp.concatenate([below, hidden], 0), ((0, 0), (0, 0), (0, 0), (1, 1), (1, 1)))
    strided = convolve(stacked, kernel_cube(kernel_two), 2, [(0, 0), (0, 0), (0, 0)], 1)
    above = passed_along(grads_cells, "space", -1)
    spread = convolve(
        jnp.concatenate([grads_cells, above], 0),
        reversed_kernel(kernel_two),
        1,
        [(1, 0), (1, 2), (1, 2)],
        2,
    )
    hidden_grads = spread.astype(jnp.bfloat16)
    local_two = weight_grad(stacked, grads_cells, 2) * scale_two
    layer_out = strided.astype(jnp.bfloat16).reshape(depth // 2, batch, channels_two, plane // 4)
    sigma = jax.nn.sigmoid(pre_one)
    pre_grads = (hidden_grads.astype(jnp.float32) * sigma * (1.0 + pre_one * (1.0 - sigma))).astype(
        jnp.bfloat16
    )
    framed_grads = with_halo(pre_grads, (("space", 0),), 1)
    input_grads = convolve(
        framed_grads, reversed_kernel(kernel_one), 1, [(0, 0), (1, 1), (1, 1)], 1
    ).astype(jnp.bfloat16)
    first_grads = first_weight_grad(framed, pre_grads) * scale_one
    first_grads, second_grads = all_sum([first_grads, local_two])
    return (
        layer_out,
        input_grads.reshape(depth, batch, channels_in, plane),
        first_grads,
        second_grads,
    )


def solution(mesh):
    in_specs = (P("space", "sample", None, None), P("space", "sample", None, None), P(), P())
    out_specs = (P("space", "sample", None, None), P("space", "sample", None, None), P(), P())
    return jax.shard_map(local, mesh=mesh, in_specs=in_specs, out_specs=out_specs, check_vma=False)
```

```python
import jax
import jax.numpy as jnp
from jax import lax
from jax.sharding import PartitionSpec as P

SIDE = 32


def with_halo(block, sides, width):
    for axis, dim in sides:
        count = lax.axis_size(axis)
        forward = [(i, i + 1) for i in range(count - 1)]
        backward = [(target, source) for source, target in forward]
        low = lax.ppermute(
            lax.slice_in_dim(block, block.shape[dim] - width, None, axis=dim), axis, forward
        )
        high = lax.ppermute(lax.slice_in_dim(block, 0, width, axis=dim), axis, backward)
        block = jnp.concatenate([low, block, high], axis=dim)
    return block


def passed_along(block, axis, distance):
    devices = range(lax.axis_size(axis))
    route = [(i - distance, i) for i in devices if i - distance in devices]
    return lax.ppermute(block, axis, route)


def convolve(inputs, kernel, stride, margins, dilation):
    return lax.conv_general_dilated(
        inputs,
        kernel,
        (stride, stride, stride),
        margins,
        lhs_dilation=(dilation, dilation, dilation),
        dimension_numbers=("DNCHW", "DHWIO", "DNCHW"),
        preferred_element_type=jnp.float32,
    )


def kernel_cube(kernel):
    return kernel.reshape(3, 3, 3, kernel.shape[1], kernel.shape[2])


def reversed_kernel(kernel):
    cube = kernel_cube(kernel)
    return jnp.transpose(cube[::-1, ::-1, ::-1], (0, 1, 2, 4, 3))


def weight_grad(padded, grads, stride):
    depth_out, rows_out, cols_out = (grads.shape[0], grads.shape[3], grads.shape[4])
    if stride == 1:
        phases = padded[None, None]
    else:
        depth, batch, channels, rows, cols = padded.shape
        phases = padded.reshape(depth, batch, channels, rows // 2, 2, cols // 2, 2)
        phases = jnp.transpose(phases, (4, 6, 0, 1, 2, 3, 5))
    windows = []
    for depth_tap in range(3):
        for row_tap in range(3):
            for col_tap in range(3):
                phase = phases[row_tap % stride, col_tap % stride]
                row0, col0 = row_tap // stride, col_tap // stride
                windows.append(
                    lax.slice(
                        phase,
                        (depth_tap, 0, 0, row0, col0),
                        (
                            depth_tap + stride * (depth_out - 1) + 1,
                            phase.shape[1],
                            phase.shape[2],
                            row0 + rows_out,
                            col0 + cols_out,
                        ),
                        (stride, 1, 1, 1, 1),
                    )
                )
    return jnp.einsum(
        "tzbiyx,zboyx->tio", jnp.stack(windows), grads, preferred_element_type=jnp.float32
    )


ROUNDS = (
    ("space", 1, 2),
    ("sample", 1, 4),
    ("sample", 4, 2),
    ("space", 8, 4),
    ("space", 2, 4),
)


def group_pairs(count, stride, radix, shift):
    pairs = []
    for i in range(count):
        g = (i // stride) % radix
        pairs.append((i, i + (((g + shift) % radix) - g) * stride))
    return pairs


def all_sum(parts):
    flat = jnp.concatenate([part.reshape(-1) for part in parts])
    rounds = []
    count = 1
    for axis, stride, radix in ROUNDS:
        if stride * radix <= lax.axis_size(axis):
            rounds.append((axis, stride, radix))
            count *= radix
    total = flat.shape[0]
    value = jnp.pad(flat, (0, -(-total // count) * count - total))
    for axis, stride, radix in rounds:
        size = lax.axis_size(axis)
        g = (lax.axis_index(axis) // stride) % radix
        chunks = value.reshape(radix, -1)
        value = lax.dynamic_index_in_dim(chunks, g, 0, keepdims=False)
        for shift in range(1, radix):
            sent = lax.dynamic_index_in_dim(chunks, (g + shift) % radix, 0, keepdims=False)
            value = value + lax.ppermute(sent, axis, group_pairs(size, stride, radix, shift))
    for axis, stride, radix in reversed(rounds):
        size = lax.axis_size(axis)
        g = (lax.axis_index(axis) // stride) % radix
        got = {
            shift: lax.ppermute(value, axis, group_pairs(size, stride, radix, shift))
            for shift in range(1, radix)
        }
        rolled = jnp.concatenate([value] + [got[radix - k] for k in range(1, radix)])
        value = jnp.roll(rolled, g * value.shape[0])
    results = []
    offset = 0
    for part in parts:
        results.append(value[offset : offset + part.size].reshape(part.shape))
        offset += part.size
    return results


def first_weight_grad(framed, grads):
    depth, batch, channels, side, _ = framed.shape
    depth_out = grads.shape[0]
    plane = side * side
    cells = jnp.transpose(framed.reshape(depth, batch, channels, plane), (2, 1, 0, 3))
    cells = jnp.pad(cells, ((0, 0), (0, 0), (0, 0), (side + 1, side + 1)))
    flat_grads = jnp.transpose(grads.reshape(depth_out, batch, -1, plane), (2, 1, 0, 3))
    column = lax.broadcasted_iota(jnp.int32, (1, 1, 1, plane), 3) % side
    per_column = []
    for col_tap in range(3):
        if col_tap == 0:
            masked = jnp.where(column == 0, 0, flat_grads)
        elif col_tap == 2:
            masked = jnp.where(column == side - 1, 0, flat_grads)
        else:
            masked = flat_grads
        windows = []
        for depth_tap in range(3):
            for row_tap in range(3):
                start = (side + 1) + (row_tap - 1) * side + (col_tap - 1)
                windows.append(
                    lax.slice(
                        cells,
                        (0, 0, depth_tap, start),
                        (channels, batch, depth_tap + depth_out, start + plane),
                    )
                )
        per_column.append(
            jnp.einsum(
                "tibzs,obzs->tio",
                jnp.stack(windows),
                masked.astype(cells.dtype),
                preferred_element_type=jnp.float32,
            )
        )
    stacked = jnp.stack(per_column, 1)
    return stacked.reshape(27, channels, -1)


def local(volume, out_grads, kernel_one, kernel_two):
    depth, batch, channels_in, plane = volume.shape
    channels_two = kernel_two.shape[2]
    half_side = SIDE // 2
    space_count = lax.axis_size("space")
    sample_count = lax.axis_size("sample")
    scale_one = float(sample_count * batch * space_count * depth * plane) ** (-0.5)
    scale_two = scale_one * 8.0**0.5
    cells = volume.reshape(depth, batch, channels_in, SIDE, SIDE)
    grads_cells = out_grads.reshape(depth // 2, batch, channels_two, half_side, half_side)
    lower = passed_along(cells[-2:], "space", 1)
    upper = passed_along(cells[:1], "space", -1)
    widened = jnp.concatenate([lower, cells, upper], 0)
    framed = widened[1:]
    pre_wide = convolve(widened, kernel_cube(kernel_one), 1, [(0, 0), (1, 1), (1, 1)], 1)
    pre_one = pre_wide[1:]
    hidden_wide = jax.nn.silu(pre_wide).astype(jnp.bfloat16)
    hidden = hidden_wide[1:]
    has_below = lax.axis_index("space") > 0
    below = jnp.where(has_below, hidden_wide[:1], jnp.zeros_like(hidden_wide[:1]))
    stacked = jnp.pad(jnp.concatenate([below, hidden], 0), ((0, 0), (0, 0), (0, 0), (1, 1), (1, 1)))
    strided = convolve(stacked, kernel_cube(kernel_two), 2, [(0, 0), (0, 0), (0, 0)], 1)
    above = passed_along(grads_cells, "space", -1)
    spread = convolve(
        jnp.concatenate([grads_cells, above], 0),
        reversed_kernel(kernel_two),
        1,
        [(1, 0), (1, 2), (1, 2)],
        2,
    )
    hidden_grads = spread.astype(jnp.bfloat16)
    local_two = weight_grad(stacked, grads_cells, 2) * scale_two
    layer_out = strided.astype(jnp.bfloat16).reshape(depth // 2, batch, channels_two, plane // 4)
    sigma = jax.nn.sigmoid(pre_one)
    pre_grads = (hidden_grads.astype(jnp.float32) * sigma * (1.0 + pre_one * (1.0 - sigma))).astype(
        jnp.bfloat16
    )
    framed_grads = with_halo(pre_grads, (("space", 0),), 1)
    input_grads = convolve(
        framed_grads, reversed_kernel(kernel_one), 1, [(0, 0), (1, 1), (1, 1)], 1
    ).astype(jnp.bfloat16)
    first_grads = first_weight_grad(framed, pre_grads) * scale_one
    first_grads, second_grads = all_sum([first_grads, local_two])
    return (
        layer_out,
        input_grads.reshape(depth, batch, channels_in, plane),
        first_grads,
        second_grads,
    )


def solution(mesh):
    in_specs = (P("space", "sample", None, None), P("space", "sample", None, None), P(), P())
    out_specs = (P("space", "sample", None, None), P("space", "sample", None, None), P(), P())
    return jax.shard_map(local, mesh=mesh, in_specs=in_specs, out_specs=out_specs, check_vma=False)
```

```python
import jax
import jax.numpy as jnp
from jax import lax
from jax.sharding import PartitionSpec as P

SIDE = 32


def with_halo(block, sides, width):
    for axis, dim in sides:
        count = lax.axis_size(axis)
        forward = [(i, i + 1) for i in range(count - 1)]
        backward = [(target, source) for source, target in forward]
        low = lax.ppermute(
            lax.slice_in_dim(block, block.shape[dim] - width, None, axis=dim), axis, forward
        )
        high = lax.ppermute(lax.slice_in_dim(block, 0, width, axis=dim), axis, backward)
        block = jnp.concatenate([low, block, high], axis=dim)
    return block


def passed_along(block, axis, distance):
    devices = range(lax.axis_size(axis))
    route = [(i - distance, i) for i in devices if i - distance in devices]
    return lax.ppermute(block, axis, route)


def convolve(inputs, kernel, stride, margins, dilation):
    return lax.conv_general_dilated(
        inputs,
        kernel,
        (stride, stride, stride),
        margins,
        lhs_dilation=(dilation, dilation, dilation),
        dimension_numbers=("DNCHW", "DHWIO", "DNCHW"),
        preferred_element_type=jnp.float32,
    )


def kernel_cube(kernel):
    return kernel.reshape(3, 3, 3, kernel.shape[1], kernel.shape[2])


def reversed_kernel(kernel):
    cube = kernel_cube(kernel)
    return jnp.transpose(cube[::-1, ::-1, ::-1], (0, 1, 2, 4, 3))


def weight_grad(padded, grads, stride):
    depth_out, rows_out, cols_out = (grads.shape[0], grads.shape[3], grads.shape[4])
    if stride == 1:
        phases = padded[None, None]
    else:
        depth, batch, channels, rows, cols = padded.shape
        phases = padded.reshape(depth, batch, channels, rows // 2, 2, cols // 2, 2)
        phases = jnp.transpose(phases, (4, 6, 0, 1, 2, 3, 5))
    windows = []
    for depth_tap in range(3):
        for row_tap in range(3):
            for col_tap in range(3):
                phase = phases[row_tap % stride, col_tap % stride]
                row0, col0 = row_tap // stride, col_tap // stride
                windows.append(
                    lax.slice(
                        phase,
                        (depth_tap, 0, 0, row0, col0),
                        (
                            depth_tap + stride * (depth_out - 1) + 1,
                            phase.shape[1],
                            phase.shape[2],
                            row0 + rows_out,
                            col0 + cols_out,
                        ),
                        (stride, 1, 1, 1, 1),
                    )
                )
    return jnp.einsum(
        "tzbiyx,zboyx->tio", jnp.stack(windows), grads, preferred_element_type=jnp.float32
    )


EXCHANGES = (("space", 1),)

ROUNDS = (
    ("sample", 1, 4),
    ("sample", 4, 2),
    ("space", 8, 4),
    ("space", 2, 4),
)


def group_pairs(count, stride, radix, shift):
    pairs = []
    for i in range(count):
        g = (i // stride) % radix
        pairs.append((i, i + (((g + shift) % radix) - g) * stride))
    return pairs


def all_sum(parts):
    flat = jnp.concatenate([part.reshape(-1) for part in parts])
    for axis, distance in EXCHANGES:
        if distance < lax.axis_size(axis):
            pairs = [(i, i ^ distance) for i in range(lax.axis_size(axis))]
            flat = flat + lax.ppermute(flat, axis, pairs)
    rounds = []
    count = 1
    for axis, stride, radix in ROUNDS:
        if stride * radix <= lax.axis_size(axis):
            rounds.append((axis, stride, radix))
            count *= radix
    total = flat.shape[0]
    value = jnp.pad(flat, (0, -(-total // count) * count - total))
    for axis, stride, radix in rounds:
        size = lax.axis_size(axis)
        g = (lax.axis_index(axis) // stride) % radix
        chunks = value.reshape(radix, -1)
        value = lax.dynamic_index_in_dim(chunks, g, 0, keepdims=False)
        for shift in range(1, radix):
            sent = lax.dynamic_index_in_dim(chunks, (g + shift) % radix, 0, keepdims=False)
            value = value + lax.ppermute(sent, axis, group_pairs(size, stride, radix, shift))
    for axis, stride, radix in reversed(rounds):
        size = lax.axis_size(axis)
        g = (lax.axis_index(axis) // stride) % radix
        got = {
            shift: lax.ppermute(value, axis, group_pairs(size, stride, radix, shift))
            for shift in range(1, radix)
        }
        rolled = jnp.concatenate([value] + [got[radix - k] for k in range(1, radix)])
        value = jnp.roll(rolled, g * value.shape[0])
    results = []
    offset = 0
    for part in parts:
        results.append(value[offset : offset + part.size].reshape(part.shape))
        offset += part.size
    return results


def first_weight_grad(framed, grads):
    depth, batch, channels, side, _ = framed.shape
    depth_out = grads.shape[0]
    plane = side * side
    cells = jnp.transpose(framed.reshape(depth, batch, channels, plane), (2, 1, 0, 3))
    cells = jnp.pad(cells, ((0, 0), (0, 0), (0, 0), (side + 1, side + 1)))
    flat_grads = jnp.transpose(grads.reshape(depth_out, batch, -1, plane), (2, 1, 0, 3))
    column = lax.broadcasted_iota(jnp.int32, (1, 1, 1, plane), 3) % side
    per_column = []
    for col_tap in range(3):
        if col_tap == 0:
            masked = jnp.where(column == 0, 0, flat_grads)
        elif col_tap == 2:
            masked = jnp.where(column == side - 1, 0, flat_grads)
        else:
            masked = flat_grads
        windows = []
        for depth_tap in range(3):
            for row_tap in range(3):
                start = (side + 1) + (row_tap - 1) * side + (col_tap - 1)
                windows.append(
                    lax.slice(
                        cells,
                        (0, 0, depth_tap, start),
                        (channels, batch, depth_tap + depth_out, start + plane),
                    )
                )
        per_column.append(
            jnp.einsum(
                "tibzs,obzs->tio",
                jnp.stack(windows),
                masked.astype(cells.dtype),
                preferred_element_type=jnp.float32,
            )
        )
    stacked = jnp.stack(per_column, 1)
    return stacked.reshape(27, channels, -1)


def local(volume, out_grads, kernel_one, kernel_two):
    depth, batch, channels_in, plane = volume.shape
    channels_two = kernel_two.shape[2]
    half_side = SIDE // 2
    space_count = lax.axis_size("space")
    sample_count = lax.axis_size("sample")
    scale_one = float(sample_count * batch * space_count * depth * plane) ** (-0.5)
    scale_two = scale_one * 8.0**0.5
    cells = volume.reshape(depth, batch, channels_in, SIDE, SIDE)
    grads_cells = out_grads.reshape(depth // 2, batch, channels_two, half_side, half_side)
    framed = with_halo(cells, (("space", 0),), 1)
    pre_one = convolve(framed, kernel_cube(kernel_one), 1, [(0, 0), (1, 1), (1, 1)], 1)
    hidden = jax.nn.silu(pre_one).astype(jnp.bfloat16)
    below = passed_along(hidden[-1:], "space", 1)
    stacked = jnp.pad(jnp.concatenate([below, hidden], 0), ((0, 0), (0, 0), (0, 0), (1, 1), (1, 1)))
    strided = convolve(stacked, kernel_cube(kernel_two), 2, [(0, 0), (0, 0), (0, 0)], 1)
    above = passed_along(grads_cells, "space", -1)
    spread = convolve(
        jnp.concatenate([grads_cells, above], 0),
        reversed_kernel(kernel_two),
        1,
        [(1, 0), (1, 2), (1, 2)],
        2,
    )
    hidden_grads = spread.astype(jnp.bfloat16)
    local_two = weight_grad(stacked, grads_cells, 2) * scale_two
    layer_out = strided.astype(jnp.bfloat16).reshape(depth // 2, batch, channels_two, plane // 4)
    sigma = jax.nn.sigmoid(pre_one)
    pre_grads = (hidden_grads.astype(jnp.float32) * sigma * (1.0 + pre_one * (1.0 - sigma))).astype(
        jnp.bfloat16
    )
    framed_grads = with_halo(pre_grads, (("space", 0),), 1)
    input_grads = convolve(
        framed_grads, reversed_kernel(kernel_one), 1, [(0, 0), (1, 1), (1, 1)], 1
    ).astype(jnp.bfloat16)
    first_grads = first_weight_grad(framed, pre_grads) * scale_one
    first_grads, second_grads = all_sum([first_grads, local_two])
    return (
        layer_out,
        input_grads.reshape(depth, batch, channels_in, plane),
        first_grads,
        second_grads,
    )


def solution(mesh):
    in_specs = (P("space", "sample", None, None), P("space", "sample", None, None), P(), P())
    out_specs = (P("space", "sample", None, None), P("space", "sample", None, None), P(), P())
    return jax.shard_map(local, mesh=mesh, in_specs=in_specs, out_specs=out_specs, check_vma=False)
```

```python
import jax
import jax.numpy as jnp
from jax import lax
from jax.sharding import PartitionSpec as P

SIDE = 32


def with_halo(block, sides, width):
    for axis, dim in sides:
        count = lax.axis_size(axis)
        forward = [(i, i + 1) for i in range(count - 1)]
        backward = [(target, source) for source, target in forward]
        low = lax.ppermute(
            lax.slice_in_dim(block, block.shape[dim] - width, None, axis=dim), axis, forward
        )
        high = lax.ppermute(lax.slice_in_dim(block, 0, width, axis=dim), axis, backward)
        block = jnp.concatenate([low, block, high], axis=dim)
    return block


def passed_along(block, axis, distance):
    devices = range(lax.axis_size(axis))
    route = [(i - distance, i) for i in devices if i - distance in devices]
    return lax.ppermute(block, axis, route)


def convolve(inputs, kernel, stride, margins, dilation):
    return lax.conv_general_dilated(
        inputs,
        kernel,
        (stride, stride, stride),
        margins,
        lhs_dilation=(dilation, dilation, dilation),
        dimension_numbers=("DNCHW", "DHWIO", "DNCHW"),
        preferred_element_type=jnp.float32,
    )


def kernel_cube(kernel):
    return kernel.reshape(3, 3, 3, kernel.shape[1], kernel.shape[2])


def reversed_kernel(kernel):
    cube = kernel_cube(kernel)
    return jnp.transpose(cube[::-1, ::-1, ::-1], (0, 1, 2, 4, 3))


def weight_grad(padded, grads, stride):
    depth_out, rows_out, cols_out = (grads.shape[0], grads.shape[3], grads.shape[4])
    if stride == 1:
        phases = padded[None, None]
    else:
        depth, batch, channels, rows, cols = padded.shape
        phases = padded.reshape(depth, batch, channels, rows // 2, 2, cols // 2, 2)
        phases = jnp.transpose(phases, (4, 6, 0, 1, 2, 3, 5))
    windows = []
    for depth_tap in range(3):
        for row_tap in range(3):
            for col_tap in range(3):
                phase = phases[row_tap % stride, col_tap % stride]
                row0, col0 = row_tap // stride, col_tap // stride
                windows.append(
                    lax.slice(
                        phase,
                        (depth_tap, 0, 0, row0, col0),
                        (
                            depth_tap + stride * (depth_out - 1) + 1,
                            phase.shape[1],
                            phase.shape[2],
                            row0 + rows_out,
                            col0 + cols_out,
                        ),
                        (stride, 1, 1, 1, 1),
                    )
                )
    return jnp.einsum(
        "tzbiyx,zboyx->tio", jnp.stack(windows), grads, preferred_element_type=jnp.float32
    )


ROUNDS = (
    ("space", 1, 2),
    ("sample", 4, 2),
    ("sample", 1, 4),
    ("space", 8, 4),
    ("space", 2, 4),
)


def group_pairs(count, stride, radix, shift):
    pairs = []
    for i in range(count):
        g = (i // stride) % radix
        pairs.append((i, i + (((g + shift) % radix) - g) * stride))
    return pairs


def all_sum(parts):
    flat = jnp.concatenate([part.reshape(-1) for part in parts])
    rounds = []
    count = 1
    for axis, stride, radix in ROUNDS:
        if stride * radix <= lax.axis_size(axis):
            rounds.append((axis, stride, radix))
            count *= radix
    total = flat.shape[0]
    value = jnp.pad(flat, (0, -(-total // count) * count - total))
    for axis, stride, radix in rounds:
        size = lax.axis_size(axis)
        g = (lax.axis_index(axis) // stride) % radix
        chunks = value.reshape(radix, -1)
        value = lax.dynamic_index_in_dim(chunks, g, 0, keepdims=False)
        for shift in range(1, radix):
            sent = lax.dynamic_index_in_dim(chunks, (g + shift) % radix, 0, keepdims=False)
            value = value + lax.ppermute(sent, axis, group_pairs(size, stride, radix, shift))
    value = value.astype(jnp.bfloat16)
    for axis, stride, radix in reversed(rounds):
        size = lax.axis_size(axis)
        g = (lax.axis_index(axis) // stride) % radix
        got = {
            shift: lax.ppermute(value, axis, group_pairs(size, stride, radix, shift))
            for shift in range(1, radix)
        }
        rolled = jnp.concatenate([value] + [got[radix - k] for k in range(1, radix)])
        value = jnp.roll(rolled, g * value.shape[0])
    value = value.astype(jnp.float32)
    results = []
    offset = 0
    for part in parts:
        results.append(value[offset : offset + part.size].reshape(part.shape))
        offset += part.size
    return results


def first_weight_grad(framed, grads):
    depth, batch, channels, side, _ = framed.shape
    depth_out = grads.shape[0]
    plane = side * side
    cells = jnp.transpose(framed.reshape(depth, batch, channels, plane), (2, 1, 0, 3))
    cells = jnp.pad(cells, ((0, 0), (0, 0), (0, 0), (side + 1, side + 1)))
    flat_grads = jnp.transpose(grads.reshape(depth_out, batch, -1, plane), (2, 1, 0, 3))
    column = lax.broadcasted_iota(jnp.int32, (1, 1, 1, plane), 3) % side
    per_column = []
    for col_tap in range(3):
        if col_tap == 0:
            masked = jnp.where(column == 0, 0, flat_grads)
        elif col_tap == 2:
            masked = jnp.where(column == side - 1, 0, flat_grads)
        else:
            masked = flat_grads
        windows = []
        for depth_tap in range(3):
            for row_tap in range(3):
                start = (side + 1) + (row_tap - 1) * side + (col_tap - 1)
                windows.append(
                    lax.slice(
                        cells,
                        (0, 0, depth_tap, start),
                        (channels, batch, depth_tap + depth_out, start + plane),
                    )
                )
        per_column.append(
            jnp.einsum(
                "tibzs,obzs->tio",
                jnp.stack(windows),
                masked.astype(cells.dtype),
                preferred_element_type=jnp.float32,
            )
        )
    stacked = jnp.stack(per_column, 1)
    return stacked.reshape(27, channels, -1)


def local(volume, out_grads, kernel_one, kernel_two):
    depth, batch, channels_in, plane = volume.shape
    channels_two = kernel_two.shape[2]
    half_side = SIDE // 2
    space_count = lax.axis_size("space")
    sample_count = lax.axis_size("sample")
    scale_one = float(sample_count * batch * space_count * depth * plane) ** (-0.5)
    scale_two = scale_one * 8.0**0.5
    cells = volume.reshape(depth, batch, channels_in, SIDE, SIDE)
    grads_cells = out_grads.reshape(depth // 2, batch, channels_two, half_side, half_side)
    framed = with_halo(cells, (("space", 0),), 1)
    pre_one = convolve(framed, kernel_cube(kernel_one), 1, [(0, 0), (1, 1), (1, 1)], 1)
    hidden = jax.nn.silu(pre_one).astype(jnp.bfloat16)
    below = passed_along(hidden[-1:], "space", 1)
    stacked = jnp.pad(jnp.concatenate([below, hidden], 0), ((0, 0), (0, 0), (0, 0), (1, 1), (1, 1)))
    strided = convolve(stacked, kernel_cube(kernel_two), 2, [(0, 0), (0, 0), (0, 0)], 1)
    above = passed_along(grads_cells, "space", -1)
    spread = convolve(
        jnp.concatenate([grads_cells, above], 0),
        reversed_kernel(kernel_two),
        1,
        [(1, 0), (1, 2), (1, 2)],
        2,
    )
    hidden_grads = spread.astype(jnp.bfloat16)
    local_two = weight_grad(stacked, grads_cells, 2) * scale_two
    layer_out = strided.astype(jnp.bfloat16).reshape(depth // 2, batch, channels_two, plane // 4)
    sigma = jax.nn.sigmoid(pre_one)
    pre_grads = (hidden_grads.astype(jnp.float32) * sigma * (1.0 + pre_one * (1.0 - sigma))).astype(
        jnp.bfloat16
    )
    framed_grads = with_halo(pre_grads, (("space", 0),), 1)
    input_grads = convolve(
        framed_grads, reversed_kernel(kernel_one), 1, [(0, 0), (1, 1), (1, 1)], 1
    ).astype(jnp.bfloat16)
    first_grads = first_weight_grad(framed, pre_grads) * scale_one
    first_grads, second_grads = all_sum([first_grads, local_two])
    return (
        layer_out,
        input_grads.reshape(depth, batch, channels_in, plane),
        first_grads,
        second_grads,
    )


def solution(mesh):
    in_specs = (P("space", "sample", None, None), P("space", "sample", None, None), P(), P())
    out_specs = (P("space", "sample", None, None), P("space", "sample", None, None), P(), P())
    return jax.shard_map(local, mesh=mesh, in_specs=in_specs, out_specs=out_specs, check_vma=False)
```

```python
import jax
import jax.numpy as jnp
from jax import lax
from jax.sharding import PartitionSpec as P

SIDE = 32


def with_halo(block, sides, width):
    for axis, dim in sides:
        count = lax.axis_size(axis)
        forward = [(i, i + 1) for i in range(count - 1)]
        backward = [(target, source) for source, target in forward]
        low = lax.ppermute(
            lax.slice_in_dim(block, block.shape[dim] - width, None, axis=dim), axis, forward
        )
        high = lax.ppermute(lax.slice_in_dim(block, 0, width, axis=dim), axis, backward)
        block = jnp.concatenate([low, block, high], axis=dim)
    return block


def passed_along(block, axis, distance):
    devices = range(lax.axis_size(axis))
    route = [(i - distance, i) for i in devices if i - distance in devices]
    return lax.ppermute(block, axis, route)


def convolve(inputs, kernel, stride, margins, dilation):
    return lax.conv_general_dilated(
        inputs,
        kernel,
        (stride, stride, stride),
        margins,
        lhs_dilation=(dilation, dilation, dilation),
        dimension_numbers=("DNCHW", "DHWIO", "DNCHW"),
        preferred_element_type=jnp.float32,
    )


def kernel_cube(kernel):
    return kernel.reshape(3, 3, 3, kernel.shape[1], kernel.shape[2])


def reversed_kernel(kernel):
    cube = kernel_cube(kernel)
    return jnp.transpose(cube[::-1, ::-1, ::-1], (0, 1, 2, 4, 3))


def weight_grad(padded, grads, stride):
    depth_out, rows_out, cols_out = (grads.shape[0], grads.shape[3], grads.shape[4])
    if stride == 1:
        phases = padded[None, None]
    else:
        depth, batch, channels, rows, cols = padded.shape
        phases = padded.reshape(depth, batch, channels, rows // 2, 2, cols // 2, 2)
        phases = jnp.transpose(phases, (4, 6, 0, 1, 2, 3, 5))
    windows = []
    for depth_tap in range(3):
        for row_tap in range(3):
            for col_tap in range(3):
                phase = phases[row_tap % stride, col_tap % stride]
                row0, col0 = row_tap // stride, col_tap // stride
                windows.append(
                    lax.slice(
                        phase,
                        (depth_tap, 0, 0, row0, col0),
                        (
                            depth_tap + stride * (depth_out - 1) + 1,
                            phase.shape[1],
                            phase.shape[2],
                            row0 + rows_out,
                            col0 + cols_out,
                        ),
                        (stride, 1, 1, 1, 1),
                    )
                )
    return jnp.einsum(
        "tzbiyx,zboyx->tio", jnp.stack(windows), grads, preferred_element_type=jnp.float32
    )


ROUNDS = (
    ("space", 1, 2),
    ("sample", 1, 4),
    ("sample", 4, 2),
    ("space", 8, 4),
    ("space", 2, 4),
)


def group_pairs(count, stride, radix, shift):
    pairs = []
    for i in range(count):
        g = (i // stride) % radix
        pairs.append((i, i + (((g + shift) % radix) - g) * stride))
    return pairs


def all_sum(parts):
    flat = jnp.concatenate([part.reshape(-1) for part in parts])
    rounds = []
    count = 1
    for axis, stride, radix in ROUNDS:
        if stride * radix <= lax.axis_size(axis):
            rounds.append((axis, stride, radix))
            count *= radix
    total = flat.shape[0]
    value = jnp.pad(flat, (0, -(-total // count) * count - total))
    for axis, stride, radix in rounds:
        size = lax.axis_size(axis)
        g = (lax.axis_index(axis) // stride) % radix
        chunks = value.reshape(radix, -1)
        value = lax.dynamic_index_in_dim(chunks, g, 0, keepdims=False)
        for shift in range(1, radix):
            sent = lax.dynamic_index_in_dim(chunks, (g + shift) % radix, 0, keepdims=False)
            value = value + lax.ppermute(sent, axis, group_pairs(size, stride, radix, shift))
    for axis, stride, radix in reversed(rounds):
        size = lax.axis_size(axis)
        g = (lax.axis_index(axis) // stride) % radix
        got = {
            shift: lax.ppermute(value, axis, group_pairs(size, stride, radix, shift))
            for shift in range(1, radix)
        }
        rolled = jnp.concatenate([value] + [got[radix - k] for k in range(1, radix)])
        value = jnp.roll(rolled, g * value.shape[0])
    results = []
    offset = 0
    for part in parts:
        results.append(value[offset : offset + part.size].reshape(part.shape))
        offset += part.size
    return results


def first_weight_grad(framed, grads):
    depth, batch, channels, side, _ = framed.shape
    depth_out = grads.shape[0]
    plane = side * side
    cells = jnp.transpose(framed.reshape(depth, batch, channels, plane), (2, 1, 0, 3))
    cells = jnp.pad(cells, ((0, 0), (0, 0), (0, 0), (side + 1, side + 1)))
    flat_grads = jnp.transpose(grads.reshape(depth_out, batch, -1, plane), (2, 1, 0, 3))
    column = lax.broadcasted_iota(jnp.int32, (1, 1, 1, plane), 3) % side
    per_column = []
    for col_tap in range(3):
        if col_tap == 0:
            masked = jnp.where(column == 0, 0, flat_grads)
        elif col_tap == 2:
            masked = jnp.where(column == side - 1, 0, flat_grads)
        else:
            masked = flat_grads
        windows = []
        for depth_tap in range(3):
            for row_tap in range(3):
                start = (side + 1) + (row_tap - 1) * side + (col_tap - 1)
                windows.append(
                    lax.slice(
                        cells,
                        (0, 0, depth_tap, start),
                        (channels, batch, depth_tap + depth_out, start + plane),
                    )
                )
        per_column.append(
            jnp.einsum(
                "tibzs,obzs->tio",
                jnp.stack(windows),
                masked.astype(cells.dtype),
                preferred_element_type=jnp.float32,
            )
        )
    stacked = jnp.stack(per_column, 1)
    return stacked.reshape(27, channels, -1)


def second_weight_grad(hidden, grads, above):
    depth, batch, channels, rows, cols = hidden.shape
    depth_out, rows_out, cols_out = (grads.shape[0], grads.shape[3], grads.shape[4])
    padded = jnp.pad(hidden, ((0, 0), (0, 0), (0, 0), (1, 1), (1, 1)))
    phases = padded.reshape(depth, batch, channels, rows // 2 + 1, 2, cols // 2 + 1, 2)
    phases = jnp.transpose(phases, (4, 6, 0, 1, 2, 3, 5))
    shifted = jnp.concatenate([grads[1:], above[:1]], 0)
    per_depth = []
    for depth_tap, first_plane, tap_grads in ((0, 1, shifted), (1, 0, grads), (2, 1, grads)):
        windows = []
        for row_tap in range(3):
            for col_tap in range(3):
                phase = phases[row_tap % 2, col_tap % 2]
                row0, col0 = row_tap // 2, col_tap // 2
                windows.append(
                    lax.slice(
                        phase,
                        (first_plane, 0, 0, row0, col0),
                        (
                            first_plane + 2 * (depth_out - 1) + 1,
                            batch,
                            channels,
                            row0 + rows_out,
                            col0 + cols_out,
                        ),
                        (2, 1, 1, 1, 1),
                    )
                )
        per_depth.append(
            jnp.einsum(
                "tzbiyx,zboyx->tio",
                jnp.stack(windows),
                tap_grads,
                preferred_element_type=jnp.float32,
            )
        )
    return jnp.stack(per_depth).reshape(27, channels, -1)


def local(volume, out_grads, kernel_one, kernel_two):
    depth, batch, channels_in, plane = volume.shape
    channels_two = kernel_two.shape[2]
    half_side = SIDE // 2
    space_count = lax.axis_size("space")
    sample_count = lax.axis_size("sample")
    scale_one = float(sample_count * batch * space_count * depth * plane) ** (-0.5)
    scale_two = scale_one * 8.0**0.5
    cells = volume.reshape(depth, batch, channels_in, SIDE, SIDE)
    grads_cells = out_grads.reshape(depth // 2, batch, channels_two, half_side, half_side)
    framed = with_halo(cells, (("space", 0),), 1)
    pre_one = convolve(framed, kernel_cube(kernel_one), 1, [(0, 0), (1, 1), (1, 1)], 1)
    hidden = jax.nn.silu(pre_one).astype(jnp.bfloat16)
    below = passed_along(hidden[-1:], "space", 1)
    stacked = jnp.pad(jnp.concatenate([below, hidden], 0), ((0, 0), (0, 0), (0, 0), (1, 1), (1, 1)))
    strided = convolve(stacked, kernel_cube(kernel_two), 2, [(0, 0), (0, 0), (0, 0)], 1)
    above = passed_along(grads_cells, "space", -1)
    spread = convolve(
        jnp.concatenate([grads_cells, above], 0),
        reversed_kernel(kernel_two),
        1,
        [(1, 0), (1, 2), (1, 2)],
        2,
    )
    hidden_grads = spread.astype(jnp.bfloat16)
    local_two = second_weight_grad(hidden, grads_cells, above) * scale_two
    layer_out = strided.astype(jnp.bfloat16).reshape(depth // 2, batch, channels_two, plane // 4)
    sigma = jax.nn.sigmoid(pre_one)
    pre_grads = (hidden_grads.astype(jnp.float32) * sigma * (1.0 + pre_one * (1.0 - sigma))).astype(
        jnp.bfloat16
    )
    framed_grads = with_halo(pre_grads, (("space", 0),), 1)
    input_grads = convolve(
        framed_grads, reversed_kernel(kernel_one), 1, [(0, 0), (1, 1), (1, 1)], 1
    ).astype(jnp.bfloat16)
    first_grads = first_weight_grad(framed, pre_grads) * scale_one
    first_grads, second_grads = all_sum([first_grads, local_two])
    return (
        layer_out,
        input_grads.reshape(depth, batch, channels_in, plane),
        first_grads,
        second_grads,
    )


def solution(mesh):
    in_specs = (P("space", "sample", None, None), P("space", "sample", None, None), P(), P())
    out_specs = (P("space", "sample", None, None), P("space", "sample", None, None), P(), P())
    return jax.shard_map(local, mesh=mesh, in_specs=in_specs, out_specs=out_specs, check_vma=False)
```

```python
import jax
import jax.numpy as jnp
from jax import lax
from jax.sharding import PartitionSpec as P

SIDE = 32


def with_halo(block, sides, width):
    for axis, dim in sides:
        count = lax.axis_size(axis)
        forward = [(i, i + 1) for i in range(count - 1)]
        backward = [(target, source) for source, target in forward]
        low = lax.ppermute(
            lax.slice_in_dim(block, block.shape[dim] - width, None, axis=dim), axis, forward
        )
        high = lax.ppermute(lax.slice_in_dim(block, 0, width, axis=dim), axis, backward)
        block = jnp.concatenate([low, block, high], axis=dim)
    return block


def passed_along(block, axis, distance):
    devices = range(lax.axis_size(axis))
    route = [(i - distance, i) for i in devices if i - distance in devices]
    return lax.ppermute(block, axis, route)


def convolve(inputs, kernel, stride, margins, dilation):
    return lax.conv_general_dilated(
        inputs,
        kernel,
        (stride, stride, stride),
        margins,
        lhs_dilation=(dilation, dilation, dilation),
        dimension_numbers=("DNCHW", "DHWIO", "DNCHW"),
        preferred_element_type=jnp.float32,
    )


def kernel_cube(kernel):
    return kernel.reshape(3, 3, 3, kernel.shape[1], kernel.shape[2])


def reversed_kernel(kernel):
    cube = kernel_cube(kernel)
    return jnp.transpose(cube[::-1, ::-1, ::-1], (0, 1, 2, 4, 3))


def weight_grad(padded, grads, stride):
    depth_out, rows_out, cols_out = (grads.shape[0], grads.shape[3], grads.shape[4])
    if stride == 1:
        phases = padded[None, None]
    else:
        depth, batch, channels, rows, cols = padded.shape
        phases = padded.reshape(depth, batch, channels, rows // 2, 2, cols // 2, 2)
        phases = jnp.transpose(phases, (4, 6, 0, 1, 2, 3, 5))
    windows = []
    for depth_tap in range(3):
        for row_tap in range(3):
            for col_tap in range(3):
                phase = phases[row_tap % stride, col_tap % stride]
                row0, col0 = row_tap // stride, col_tap // stride
                windows.append(
                    lax.slice(
                        phase,
                        (depth_tap, 0, 0, row0, col0),
                        (
                            depth_tap + stride * (depth_out - 1) + 1,
                            phase.shape[1],
                            phase.shape[2],
                            row0 + rows_out,
                            col0 + cols_out,
                        ),
                        (stride, 1, 1, 1, 1),
                    )
                )
    return jnp.einsum(
        "tzbiyx,zboyx->tio", jnp.stack(windows), grads, preferred_element_type=jnp.float32
    )


ROUNDS = (
    ("space", 1, 2),
    ("sample", 1, 4),
    ("sample", 4, 2),
    ("space", 8, 4),
    ("space", 2, 4),
)


def group_pairs(count, stride, radix, shift):
    pairs = []
    for i in range(count):
        g = (i // stride) % radix
        pairs.append((i, i + (((g + shift) % radix) - g) * stride))
    return pairs


def picked(g, chunks, shift):
    radix = len(chunks)
    out = chunks[shift % radix]
    for k in range(1, radix):
        out = jnp.where(g == k, chunks[(k + shift) % radix], out)
    return out


def all_sum(parts):
    flat = jnp.concatenate([part.reshape(-1) for part in parts])
    rounds = []
    count = 1
    for axis, stride, radix in ROUNDS:
        if stride * radix <= lax.axis_size(axis):
            rounds.append((axis, stride, radix))
            count *= radix
    total = flat.shape[0]
    value = jnp.pad(flat, (0, -(-total // count) * count - total))
    for axis, stride, radix in rounds:
        size = lax.axis_size(axis)
        g = (lax.axis_index(axis) // stride) % radix
        chunks = jnp.split(value, radix)
        value = picked(g, chunks, 0)
        for shift in range(1, radix):
            sent = picked(g, chunks, shift)
            value = value + lax.ppermute(sent, axis, group_pairs(size, stride, radix, shift))
    for axis, stride, radix in reversed(rounds):
        size = lax.axis_size(axis)
        g = (lax.axis_index(axis) // stride) % radix
        got = [value] + [
            lax.ppermute(value, axis, group_pairs(size, stride, radix, shift))
            for shift in range(1, radix)
        ]
        pieces = []
        for place in range(radix):
            piece = got[(radix - place) % radix]
            for shift in range(radix):
                piece = jnp.where(g == (place + shift) % radix, got[shift], piece)
            pieces.append(piece)
        value = jnp.concatenate(pieces)
    results = []
    offset = 0
    for part in parts:
        results.append(value[offset : offset + part.size].reshape(part.shape))
        offset += part.size
    return results


def first_weight_grad(framed, grads):
    depth, batch, channels, side, _ = framed.shape
    depth_out = grads.shape[0]
    plane = side * side
    cells = jnp.transpose(framed.reshape(depth, batch, channels, plane), (2, 1, 0, 3))
    cells = jnp.pad(cells, ((0, 0), (0, 0), (0, 0), (side + 1, side + 1)))
    flat_grads = jnp.transpose(grads.reshape(depth_out, batch, -1, plane), (2, 1, 0, 3))
    column = lax.broadcasted_iota(jnp.int32, (1, 1, 1, plane), 3) % side
    per_column = []
    for col_tap in range(3):
        if col_tap == 0:
            masked = jnp.where(column == 0, 0, flat_grads)
        elif col_tap == 2:
            masked = jnp.where(column == side - 1, 0, flat_grads)
        else:
            masked = flat_grads
        windows = []
        for depth_tap in range(3):
            for row_tap in range(3):
                start = (side + 1) + (row_tap - 1) * side + (col_tap - 1)
                windows.append(
                    lax.slice(
                        cells,
                        (0, 0, depth_tap, start),
                        (channels, batch, depth_tap + depth_out, start + plane),
                    )
                )
        per_column.append(
            jnp.einsum(
                "tibzs,obzs->tio",
                jnp.stack(windows),
                masked.astype(cells.dtype),
                preferred_element_type=jnp.float32,
            )
        )
    stacked = jnp.stack(per_column, 1)
    return stacked.reshape(27, channels, -1)


def local(volume, out_grads, kernel_one, kernel_two):
    depth, batch, channels_in, plane = volume.shape
    channels_two = kernel_two.shape[2]
    half_side = SIDE // 2
    space_count = lax.axis_size("space")
    sample_count = lax.axis_size("sample")
    scale_one = float(sample_count * batch * space_count * depth * plane) ** (-0.5)
    scale_two = scale_one * 8.0**0.5
    cells = volume.reshape(depth, batch, channels_in, SIDE, SIDE)
    grads_cells = out_grads.reshape(depth // 2, batch, channels_two, half_side, half_side)
    framed = with_halo(cells, (("space", 0),), 1)
    pre_one = convolve(framed, kernel_cube(kernel_one), 1, [(0, 0), (1, 1), (1, 1)], 1)
    hidden = jax.nn.silu(pre_one).astype(jnp.bfloat16)
    below = passed_along(hidden[-1:], "space", 1)
    stacked = jnp.pad(jnp.concatenate([below, hidden], 0), ((0, 0), (0, 0), (0, 0), (1, 1), (1, 1)))
    strided = convolve(stacked, kernel_cube(kernel_two), 2, [(0, 0), (0, 0), (0, 0)], 1)
    above = passed_along(grads_cells, "space", -1)
    spread = convolve(
        jnp.concatenate([grads_cells, above], 0),
        reversed_kernel(kernel_two),
        1,
        [(1, 0), (1, 2), (1, 2)],
        2,
    )
    hidden_grads = spread.astype(jnp.bfloat16)
    local_two = weight_grad(stacked, grads_cells, 2) * scale_two
    layer_out = strided.astype(jnp.bfloat16).reshape(depth // 2, batch, channels_two, plane // 4)
    sigma = jax.nn.sigmoid(pre_one)
    pre_grads = (hidden_grads.astype(jnp.float32) * sigma * (1.0 + pre_one * (1.0 - sigma))).astype(
        jnp.bfloat16
    )
    framed_grads = with_halo(pre_grads, (("space", 0),), 1)
    input_grads = convolve(
        framed_grads, reversed_kernel(kernel_one), 1, [(0, 0), (1, 1), (1, 1)], 1
    ).astype(jnp.bfloat16)
    first_grads = first_weight_grad(framed, pre_grads) * scale_one
    first_grads, second_grads = all_sum([first_grads, local_two])
    return (
        layer_out,
        input_grads.reshape(depth, batch, channels_in, plane),
        first_grads,
        second_grads,
    )


def solution(mesh):
    in_specs = (P("space", "sample", None, None), P("space", "sample", None, None), P(), P())
    out_specs = (P("space", "sample", None, None), P("space", "sample", None, None), P(), P())
    return jax.shard_map(local, mesh=mesh, in_specs=in_specs, out_specs=out_specs, check_vma=False)
```

```python
import jax
import jax.numpy as jnp
from jax import lax
from jax.sharding import PartitionSpec as P

SIDE = 32


def with_halo(block, sides, width):
    for axis, dim in sides:
        count = lax.axis_size(axis)
        forward = [(i, i + 1) for i in range(count - 1)]
        backward = [(target, source) for source, target in forward]
        low = lax.ppermute(
            lax.slice_in_dim(block, block.shape[dim] - width, None, axis=dim), axis, forward
        )
        high = lax.ppermute(lax.slice_in_dim(block, 0, width, axis=dim), axis, backward)
        block = jnp.concatenate([low, block, high], axis=dim)
    return block


def passed_along(block, axis, distance):
    devices = range(lax.axis_size(axis))
    route = [(i - distance, i) for i in devices if i - distance in devices]
    return lax.ppermute(block, axis, route)


def convolve(inputs, kernel, stride, margins, dilation):
    return lax.conv_general_dilated(
        inputs,
        kernel,
        (stride, stride, stride),
        margins,
        lhs_dilation=(dilation, dilation, dilation),
        dimension_numbers=("DNCHW", "DHWIO", "DNCHW"),
        preferred_element_type=jnp.float32,
    )


def kernel_cube(kernel):
    return kernel.reshape(3, 3, 3, kernel.shape[1], kernel.shape[2])


def reversed_kernel(kernel):
    cube = kernel_cube(kernel)
    return jnp.transpose(cube[::-1, ::-1, ::-1], (0, 1, 2, 4, 3))


def tap_windows(padded, stride, depth_out, rows_out, cols_out):
    if stride == 1:
        phases = padded[None, None]
    else:
        depth, batch, channels, rows, cols = padded.shape
        phases = padded.reshape(depth, batch, channels, rows // 2, 2, cols // 2, 2)
        phases = jnp.transpose(phases, (4, 6, 0, 1, 2, 3, 5))
    windows = []
    for depth_tap in range(3):
        for row_tap in range(3):
            for col_tap in range(3):
                phase = phases[row_tap % stride, col_tap % stride]
                row0, col0 = row_tap // stride, col_tap // stride
                windows.append(
                    lax.slice(
                        phase,
                        (depth_tap, 0, 0, row0, col0),
                        (
                            depth_tap + stride * (depth_out - 1) + 1,
                            phase.shape[1],
                            phase.shape[2],
                            row0 + rows_out,
                            col0 + cols_out,
                        ),
                        (stride, 1, 1, 1, 1),
                    )
                )
    return jnp.stack(windows)


ROUNDS = (
    ("space", 1, 2),
    ("sample", 1, 4),
    ("sample", 4, 2),
    ("space", 8, 4),
    ("space", 2, 4),
)


def group_pairs(count, stride, radix, shift):
    pairs = []
    for i in range(count):
        g = (i // stride) % radix
        pairs.append((i, i + (((g + shift) % radix) - g) * stride))
    return pairs


def picked(g, chunks, shift):
    radix = len(chunks)
    out = chunks[shift % radix]
    for k in range(1, radix):
        out = jnp.where(g == k, chunks[(k + shift) % radix], out)
    return out


def all_sum(parts):
    flat = jnp.concatenate([part.reshape(-1) for part in parts])
    rounds = []
    count = 1
    for axis, stride, radix in ROUNDS:
        if stride * radix <= lax.axis_size(axis):
            rounds.append((axis, stride, radix))
            count *= radix
    total = flat.shape[0]
    value = jnp.pad(flat, (0, -(-total // count) * count - total))
    for axis, stride, radix in rounds:
        size = lax.axis_size(axis)
        g = (lax.axis_index(axis) // stride) % radix
        chunks = jnp.split(value, radix)
        value = picked(g, chunks, 0)
        for shift in range(1, radix):
            sent = picked(g, chunks, shift)
            value = value + lax.ppermute(sent, axis, group_pairs(size, stride, radix, shift))
    for axis, stride, radix in reversed(rounds):
        size = lax.axis_size(axis)
        g = (lax.axis_index(axis) // stride) % radix
        got = [value] + [
            lax.ppermute(value, axis, group_pairs(size, stride, radix, shift))
            for shift in range(1, radix)
        ]
        pieces = []
        for place in range(radix):
            piece = got[(radix - place) % radix]
            for shift in range(radix):
                piece = jnp.where(g == (place + shift) % radix, got[shift], piece)
            pieces.append(piece)
        value = jnp.concatenate(pieces)
    results = []
    offset = 0
    for part in parts:
        results.append(value[offset : offset + part.size].reshape(part.shape))
        offset += part.size
    return results


def first_weight_grad(framed, grads):
    depth, batch, channels, side, _ = framed.shape
    depth_out = grads.shape[0]
    plane = side * side
    cells = jnp.transpose(framed.reshape(depth, batch, channels, plane), (2, 1, 0, 3))
    cells = jnp.pad(cells, ((0, 0), (0, 0), (0, 0), (side + 1, side + 1)))
    flat_grads = jnp.transpose(grads.reshape(depth_out, batch, -1, plane), (2, 1, 0, 3))
    column = lax.broadcasted_iota(jnp.int32, (1, 1, 1, plane), 3) % side
    per_column = []
    for col_tap in range(3):
        if col_tap == 0:
            masked = jnp.where(column == 0, 0, flat_grads)
        elif col_tap == 2:
            masked = jnp.where(column == side - 1, 0, flat_grads)
        else:
            masked = flat_grads
        windows = []
        for depth_tap in range(3):
            for row_tap in range(3):
                start = (side + 1) + (row_tap - 1) * side + (col_tap - 1)
                windows.append(
                    lax.slice(
                        cells,
                        (0, 0, depth_tap, start),
                        (channels, batch, depth_tap + depth_out, start + plane),
                    )
                )
        per_column.append(
            jnp.einsum(
                "tibzs,obzs->tio",
                jnp.stack(windows),
                masked.astype(cells.dtype),
                preferred_element_type=jnp.float32,
            )
        )
    stacked = jnp.stack(per_column, 1)
    return stacked.reshape(27, channels, -1)


def local(volume, out_grads, kernel_one, kernel_two):
    depth, batch, channels_in, plane = volume.shape
    channels_two = kernel_two.shape[2]
    half_side = SIDE // 2
    space_count = lax.axis_size("space")
    sample_count = lax.axis_size("sample")
    scale_one = float(sample_count * batch * space_count * depth * plane) ** (-0.5)
    scale_two = scale_one * 8.0**0.5
    cells = volume.reshape(depth, batch, channels_in, SIDE, SIDE)
    grads_cells = out_grads.reshape(depth // 2, batch, channels_two, half_side, half_side)
    framed = with_halo(cells, (("space", 0),), 1)
    pre_one = convolve(framed, kernel_cube(kernel_one), 1, [(0, 0), (1, 1), (1, 1)], 1)
    hidden = jax.nn.silu(pre_one).astype(jnp.bfloat16)
    below = passed_along(hidden[-1:], "space", 1)
    stacked = jnp.pad(jnp.concatenate([below, hidden], 0), ((0, 0), (0, 0), (0, 0), (1, 1), (1, 1)))
    windows_two = tap_windows(
        stacked, 2, depth // 2, half_side, half_side
    )
    strided = jnp.einsum(
        "tzbiyx,tio->zboyx", windows_two, kernel_two, preferred_element_type=jnp.float32
    )
    above = passed_along(grads_cells, "space", -1)
    spread = convolve(
        jnp.concatenate([grads_cells, above], 0),
        reversed_kernel(kernel_two),
        1,
        [(1, 0), (1, 2), (1, 2)],
        2,
    )
    hidden_grads = spread.astype(jnp.bfloat16)
    local_two = jnp.einsum(
        "tzbiyx,zboyx->tio", windows_two, grads_cells, preferred_element_type=jnp.float32
    ) * scale_two
    layer_out = strided.astype(jnp.bfloat16).reshape(depth // 2, batch, channels_two, plane // 4)
    sigma = jax.nn.sigmoid(pre_one)
    pre_grads = (hidden_grads.astype(jnp.float32) * sigma * (1.0 + pre_one * (1.0 - sigma))).astype(
        jnp.bfloat16
    )
    framed_grads = with_halo(pre_grads, (("space", 0),), 1)
    input_grads = convolve(
        framed_grads, reversed_kernel(kernel_one), 1, [(0, 0), (1, 1), (1, 1)], 1
    ).astype(jnp.bfloat16)
    first_grads = first_weight_grad(framed, pre_grads) * scale_one
    first_grads, second_grads = all_sum([first_grads, local_two])
    return (
        layer_out,
        input_grads.reshape(depth, batch, channels_in, plane),
        first_grads,
        second_grads,
    )


def solution(mesh):
    in_specs = (P("space", "sample", None, None), P("space", "sample", None, None), P(), P())
    out_specs = (P("space", "sample", None, None), P("space", "sample", None, None), P(), P())
    return jax.shard_map(local, mesh=mesh, in_specs=in_specs, out_specs=out_specs, check_vma=False)
```

```python
import jax
import jax.numpy as jnp
from jax import lax
from jax.sharding import PartitionSpec as P

SIDE = 32


def with_halo(block, sides, width):
    for axis, dim in sides:
        count = lax.axis_size(axis)
        forward = [(i, i + 1) for i in range(count - 1)]
        backward = [(target, source) for source, target in forward]
        low = lax.ppermute(
            lax.slice_in_dim(block, block.shape[dim] - width, None, axis=dim), axis, forward
        )
        high = lax.ppermute(lax.slice_in_dim(block, 0, width, axis=dim), axis, backward)
        block = jnp.concatenate([low, block, high], axis=dim)
    return block


def passed_along(block, axis, distance):
    devices = range(lax.axis_size(axis))
    route = [(i - distance, i) for i in devices if i - distance in devices]
    return lax.ppermute(block, axis, route)


def convolve(inputs, kernel, stride, margins, dilation):
    return lax.conv_general_dilated(
        inputs,
        kernel,
        (stride, stride, stride),
        margins,
        lhs_dilation=(dilation, dilation, dilation),
        dimension_numbers=("DNCHW", "DHWIO", "DNCHW"),
        preferred_element_type=jnp.float32,
    )


def kernel_cube(kernel):
    return kernel.reshape(3, 3, 3, kernel.shape[1], kernel.shape[2])


def reversed_kernel(kernel):
    cube = kernel_cube(kernel)
    return jnp.transpose(cube[::-1, ::-1, ::-1], (0, 1, 2, 4, 3))


def tap_windows(padded, stride, depth_out, rows_out, cols_out):
    if stride == 1:
        phases = padded[None, None]
    else:
        depth, batch, channels, rows, cols = padded.shape
        phases = padded.reshape(depth, batch, channels, rows // 2, 2, cols // 2, 2)
        phases = jnp.transpose(phases, (4, 6, 0, 1, 2, 3, 5))
    windows = []
    for depth_tap in range(3):
        for row_tap in range(3):
            for col_tap in range(3):
                phase = phases[row_tap % stride, col_tap % stride]
                row0, col0 = row_tap // stride, col_tap // stride
                windows.append(
                    lax.slice(
                        phase,
                        (depth_tap, 0, 0, row0, col0),
                        (
                            depth_tap + stride * (depth_out - 1) + 1,
                            phase.shape[1],
                            phase.shape[2],
                            row0 + rows_out,
                            col0 + cols_out,
                        ),
                        (stride, 1, 1, 1, 1),
                    )
                )
    return jnp.stack(windows)


ROUNDS = (
    ("space", 1, 2),
    ("sample", 1, 4),
    ("sample", 4, 2),
    ("space", 8, 4),
    ("space", 2, 4),
)


def group_pairs(count, stride, radix, shift):
    pairs = []
    for i in range(count):
        g = (i // stride) % radix
        pairs.append((i, i + (((g + shift) % radix) - g) * stride))
    return pairs


def picked(g, chunks, shift):
    radix = len(chunks)
    out = chunks[shift % radix]
    for k in range(1, radix):
        out = jnp.where(g == k, chunks[(k + shift) % radix], out)
    return out


def all_sum(parts):
    flat = jnp.concatenate([part.reshape(-1) for part in parts])
    rounds = []
    count = 1
    for axis, stride, radix in ROUNDS:
        if stride * radix <= lax.axis_size(axis):
            rounds.append((axis, stride, radix))
            count *= radix
    total = flat.shape[0]
    value = jnp.pad(flat, (0, -(-total // count) * count - total))
    for axis, stride, radix in rounds:
        size = lax.axis_size(axis)
        g = (lax.axis_index(axis) // stride) % radix
        chunks = jnp.split(value, radix)
        value = picked(g, chunks, 0)
        for shift in range(1, radix):
            sent = picked(g, chunks, shift)
            value = value + lax.ppermute(sent, axis, group_pairs(size, stride, radix, shift))
    for axis, stride, radix in reversed(rounds):
        size = lax.axis_size(axis)
        g = (lax.axis_index(axis) // stride) % radix
        got = [value] + [
            lax.ppermute(value, axis, group_pairs(size, stride, radix, shift))
            for shift in range(1, radix)
        ]
        pieces = []
        for place in range(radix):
            piece = got[(radix - place) % radix]
            for shift in range(radix):
                piece = jnp.where(g == (place + shift) % radix, got[shift], piece)
            pieces.append(piece)
        value = jnp.concatenate(pieces)
    results = []
    offset = 0
    for part in parts:
        results.append(value[offset : offset + part.size].reshape(part.shape))
        offset += part.size
    return results


def column_windows(framed, depth_out):
    depth, batch, channels, side, _ = framed.shape
    plane = side * side
    cells = jnp.transpose(framed.reshape(depth, batch, channels, plane), (2, 1, 0, 3))
    cells = jnp.pad(cells, ((0, 0), (0, 0), (0, 0), (side + 1, side + 1)))
    stacks = []
    for col_tap in range(3):
        windows = []
        for depth_tap in range(3):
            for row_tap in range(3):
                start = (side + 1) + (row_tap - 1) * side + (col_tap - 1)
                windows.append(
                    lax.slice(
                        cells,
                        (0, 0, depth_tap, start),
                        (channels, batch, depth_tap + depth_out, start + plane),
                    )
                )
        stacks.append(jnp.stack(windows))
    return stacks


def edge_masked(values, col_tap, side):
    column = lax.broadcasted_iota(jnp.int32, values.shape, values.ndim - 1) % side
    if col_tap == 0:
        return jnp.where(column == 0, 0, values)
    if col_tap == 2:
        return jnp.where(column == side - 1, 0, values)
    return values


def first_forward(stacks, kernel, side):
    cube = kernel_cube(kernel)
    total = None
    for col_tap in range(3):
        taps = cube[:, :, col_tap].reshape(9, kernel.shape[1], kernel.shape[2])
        part = jnp.einsum("tibzs,tio->zbos", stacks[col_tap], taps, preferred_element_type=jnp.float32)
        part = edge_masked(part, col_tap, side)
        total = part if total is None else total + part
    return total.reshape(total.shape[:3] + (side, side))


def first_weight_grad(stacks, grads):
    depth_out, batch, channels_out, side, _ = grads.shape
    flat_grads = jnp.transpose(grads.reshape(depth_out, batch, channels_out, side * side), (2, 1, 0, 3))
    per_column = []
    for col_tap in range(3):
        masked = edge_masked(flat_grads, col_tap, side)
        per_column.append(
            jnp.einsum(
                "tibzs,obzs->tio",
                stacks[col_tap],
                masked.astype(stacks[col_tap].dtype),
                preferred_element_type=jnp.float32,
            )
        )
    stacked = jnp.stack(per_column, 1)
    return stacked.reshape(27, stacked.shape[2], -1)


def local(volume, out_grads, kernel_one, kernel_two):
    depth, batch, channels_in, plane = volume.shape
    channels_two = kernel_two.shape[2]
    half_side = SIDE // 2
    space_count = lax.axis_size("space")
    sample_count = lax.axis_size("sample")
    scale_one = float(sample_count * batch * space_count * depth * plane) ** (-0.5)
    scale_two = scale_one * 8.0**0.5
    cells = volume.reshape(depth, batch, channels_in, SIDE, SIDE)
    grads_cells = out_grads.reshape(depth // 2, batch, channels_two, half_side, half_side)
    framed = with_halo(cells, (("space", 0),), 1)
    stacks_one = column_windows(framed, depth)
    pre_one = first_forward(stacks_one, kernel_one, SIDE)
    hidden = jax.nn.silu(pre_one).astype(jnp.bfloat16)
    below = passed_along(hidden[-1:], "space", 1)
    stacked = jnp.pad(jnp.concatenate([below, hidden], 0), ((0, 0), (0, 0), (0, 0), (1, 1), (1, 1)))
    windows_two = tap_windows(
        stacked, 2, depth // 2, half_side, half_side
    )
    strided = jnp.einsum(
        "tzbiyx,tio->zboyx", windows_two, kernel_two, preferred_element_type=jnp.float32
    )
    above = passed_along(grads_cells, "space", -1)
    spread = convolve(
        jnp.concatenate([grads_cells, above], 0),
        reversed_kernel(kernel_two),
        1,
        [(1, 0), (1, 2), (1, 2)],
        2,
    )
    hidden_grads = spread.astype(jnp.bfloat16)
    local_two = jnp.einsum(
        "tzbiyx,zboyx->tio", windows_two, grads_cells, preferred_element_type=jnp.float32
    ) * scale_two
    layer_out = strided.astype(jnp.bfloat16).reshape(depth // 2, batch, channels_two, plane // 4)
    sigma = jax.nn.sigmoid(pre_one)
    pre_grads = (hidden_grads.astype(jnp.float32) * sigma * (1.0 + pre_one * (1.0 - sigma))).astype(
        jnp.bfloat16
    )
    framed_grads = with_halo(pre_grads, (("space", 0),), 1)
    input_grads = convolve(
        framed_grads, reversed_kernel(kernel_one), 1, [(0, 0), (1, 1), (1, 1)], 1
    ).astype(jnp.bfloat16)
    first_grads = first_weight_grad(stacks_one, pre_grads) * scale_one
    first_grads, second_grads = all_sum([first_grads, local_two])
    return (
        layer_out,
        input_grads.reshape(depth, batch, channels_in, plane),
        first_grads,
        second_grads,
    )


def solution(mesh):
    in_specs = (P("space", "sample", None, None), P("space", "sample", None, None), P(), P())
    out_specs = (P("space", "sample", None, None), P("space", "sample", None, None), P(), P())
    return jax.shard_map(local, mesh=mesh, in_specs=in_specs, out_specs=out_specs, check_vma=False)
```

```python
import jax
import jax.numpy as jnp
from jax import lax
from jax.sharding import PartitionSpec as P

SIDE = 32


def with_halo(block, sides, width):
    for axis, dim in sides:
        count = lax.axis_size(axis)
        forward = [(i, i + 1) for i in range(count - 1)]
        backward = [(target, source) for source, target in forward]
        low = lax.ppermute(
            lax.slice_in_dim(block, block.shape[dim] - width, None, axis=dim), axis, forward
        )
        high = lax.ppermute(lax.slice_in_dim(block, 0, width, axis=dim), axis, backward)
        block = jnp.concatenate([low, block, high], axis=dim)
    return block


def passed_along(block, axis, distance):
    devices = range(lax.axis_size(axis))
    route = [(i - distance, i) for i in devices if i - distance in devices]
    return lax.ppermute(block, axis, route)


def convolve(inputs, kernel, stride, margins, dilation):
    return lax.conv_general_dilated(
        inputs,
        kernel,
        (stride, stride, stride),
        margins,
        lhs_dilation=(dilation, dilation, dilation),
        dimension_numbers=("DNCHW", "DHWIO", "DNCHW"),
        preferred_element_type=jnp.float32,
    )


def kernel_cube(kernel):
    return kernel.reshape(3, 3, 3, kernel.shape[1], kernel.shape[2])


def reversed_kernel(kernel):
    cube = kernel_cube(kernel)
    return jnp.transpose(cube[::-1, ::-1, ::-1], (0, 1, 2, 4, 3))


def tap_windows(padded, stride, depth_out, rows_out, cols_out):
    if stride == 1:
        phases = padded[None, None]
    else:
        depth, batch, channels, rows, cols = padded.shape
        phases = padded.reshape(depth, batch, channels, rows // 2, 2, cols // 2, 2)
        phases = jnp.transpose(phases, (4, 6, 0, 1, 2, 3, 5))
    windows = []
    for depth_tap in range(3):
        for row_tap in range(3):
            for col_tap in range(3):
                phase = phases[row_tap % stride, col_tap % stride]
                row0, col0 = row_tap // stride, col_tap // stride
                windows.append(
                    lax.slice(
                        phase,
                        (depth_tap, 0, 0, row0, col0),
                        (
                            depth_tap + stride * (depth_out - 1) + 1,
                            phase.shape[1],
                            phase.shape[2],
                            row0 + rows_out,
                            col0 + cols_out,
                        ),
                        (stride, 1, 1, 1, 1),
                    )
                )
    return jnp.stack(windows)


ROUNDS = (
    ("space", 1, 2),
    ("sample", 1, 4),
    ("sample", 4, 2),
    ("space", 8, 4),
    ("space", 2, 4),
)


def group_pairs(count, stride, radix, shift):
    pairs = []
    for i in range(count):
        g = (i // stride) % radix
        pairs.append((i, i + (((g + shift) % radix) - g) * stride))
    return pairs


def picked(g, chunks, shift):
    radix = len(chunks)
    out = chunks[shift % radix]
    for k in range(1, radix):
        out = jnp.where(g == k, chunks[(k + shift) % radix], out)
    return out


def all_sum(parts):
    flat = jnp.concatenate([part.reshape(-1) for part in parts])
    rounds = []
    count = 1
    for axis, stride, radix in ROUNDS:
        if stride * radix <= lax.axis_size(axis):
            rounds.append((axis, stride, radix))
            count *= radix
    total = flat.shape[0]
    value = jnp.pad(flat, (0, -(-total // count) * count - total))
    for axis, stride, radix in rounds:
        size = lax.axis_size(axis)
        g = (lax.axis_index(axis) // stride) % radix
        chunks = jnp.split(value, radix)
        value = picked(g, chunks, 0)
        for shift in range(1, radix):
            sent = picked(g, chunks, shift)
            value = value + lax.ppermute(sent, axis, group_pairs(size, stride, radix, shift))
    for axis, stride, radix in reversed(rounds):
        size = lax.axis_size(axis)
        g = (lax.axis_index(axis) // stride) % radix
        got = [value] + [
            lax.ppermute(value, axis, group_pairs(size, stride, radix, shift))
            for shift in range(1, radix)
        ]
        pieces = []
        for place in range(radix):
            piece = got[(radix - place) % radix]
            for shift in range(radix):
                piece = jnp.where(g == (place + shift) % radix, got[shift], piece)
            pieces.append(piece)
        value = jnp.concatenate(pieces)
    results = []
    offset = 0
    for part in parts:
        results.append(value[offset : offset + part.size].reshape(part.shape))
        offset += part.size
    return results


def column_windows(framed, depth_out):
    depth, batch, channels, side, _ = framed.shape
    plane = side * side
    cells = jnp.transpose(framed.reshape(depth, batch, channels, plane), (2, 1, 0, 3))
    cells = jnp.pad(cells, ((0, 0), (0, 0), (0, 0), (side + 1, side + 1)))
    stacks = []
    for col_tap in range(3):
        windows = []
        for depth_tap in range(3):
            for row_tap in range(3):
                start = (side + 1) + (row_tap - 1) * side + (col_tap - 1)
                windows.append(
                    lax.slice(
                        cells,
                        (0, 0, depth_tap, start),
                        (channels, batch, depth_tap + depth_out, start + plane),
                    )
                )
        stacks.append(jnp.stack(windows))
    return stacks


def edge_masked(values, col_tap, side):
    column = lax.broadcasted_iota(jnp.int32, values.shape, values.ndim - 1) % side
    if col_tap == 0:
        return jnp.where(column == 0, 0, values)
    if col_tap == 2:
        return jnp.where(column == side - 1, 0, values)
    return values


def first_forward(stacks, kernel, side):
    cube = kernel_cube(kernel)
    total = None
    for col_tap in range(3):
        taps = cube[:, :, col_tap].reshape(9, kernel.shape[1], kernel.shape[2])
        part = jnp.einsum("tibzs,tio->zbos", stacks[col_tap], taps, preferred_element_type=jnp.float32)
        part = edge_masked(part, col_tap, side)
        total = part if total is None else total + part
    return total.reshape(total.shape[:3] + (side, side))


def first_weight_grad(stacks, grads):
    depth_out, batch, channels_out, side, _ = grads.shape
    flat_grads = jnp.transpose(grads.reshape(depth_out, batch, channels_out, side * side), (2, 1, 0, 3))
    per_column = []
    for col_tap in range(3):
        masked = edge_masked(flat_grads, col_tap, side)
        per_column.append(
            jnp.einsum(
                "tibzs,obzs->tio",
                stacks[col_tap],
                masked.astype(stacks[col_tap].dtype),
                preferred_element_type=jnp.float32,
            )
        )
    stacked = jnp.stack(per_column, 1)
    return stacked.reshape(27, stacked.shape[2], -1)


def local(volume, out_grads, kernel_one, kernel_two):
    depth, batch, channels_in, plane = volume.shape
    channels_two = kernel_two.shape[2]
    half_side = SIDE // 2
    space_count = lax.axis_size("space")
    sample_count = lax.axis_size("sample")
    scale_one = float(sample_count * batch * space_count * depth * plane) ** (-0.5)
    scale_two = scale_one * 8.0**0.5
    cells = volume.reshape(depth, batch, channels_in, SIDE, SIDE)
    grads_cells = out_grads.reshape(depth // 2, batch, channels_two, half_side, half_side)
    framed = with_halo(cells, (("space", 0),), 1)
    stacks_one = column_windows(framed, depth)
    pre_one = first_forward(stacks_one, kernel_one, SIDE)
    hidden = jax.nn.silu(pre_one).astype(jnp.bfloat16)
    below = passed_along(hidden[-1:], "space", 1)
    stacked = jnp.pad(jnp.concatenate([below, hidden], 0), ((0, 0), (0, 0), (0, 0), (1, 1), (1, 1)))
    windows_two = tap_windows(
        stacked, 2, depth // 2, half_side, half_side
    )
    strided = jnp.einsum(
        "tzbiyx,tio->zboyx", windows_two, kernel_two, preferred_element_type=jnp.float32
    )
    above = passed_along(grads_cells, "space", -1)
    spread = convolve(
        jnp.concatenate([grads_cells, above], 0),
        reversed_kernel(kernel_two),
        1,
        [(1, 0), (1, 2), (1, 2)],
        2,
    )
    hidden_grads = spread.astype(jnp.bfloat16)
    local_two = jnp.einsum(
        "tzbiyx,zboyx->tio", windows_two, grads_cells, preferred_element_type=jnp.float32
    ) * scale_two
    layer_out = strided.astype(jnp.bfloat16).reshape(depth // 2, batch, channels_two, plane // 4)
    sigma = jax.nn.sigmoid(pre_one)
    pre_grads = (hidden_grads.astype(jnp.float32) * sigma * (1.0 + pre_one * (1.0 - sigma))).astype(
        jnp.bfloat16
    )
    framed_grads = with_halo(pre_grads, (("space", 0),), 1)
    flipped = reversed_kernel(kernel_one).reshape(27, kernel_one.shape[2], kernel_one.shape[1])
    input_grads = first_forward(column_windows(framed_grads, depth), flipped, SIDE).astype(
        jnp.bfloat16
    )
    first_grads = first_weight_grad(stacks_one, pre_grads) * scale_one
    first_grads, second_grads = all_sum([first_grads, local_two])
    return (
        layer_out,
        input_grads.reshape(depth, batch, channels_in, plane),
        first_grads,
        second_grads,
    )


def solution(mesh):
    in_specs = (P("space", "sample", None, None), P("space", "sample", None, None), P(), P())
    out_specs = (P("space", "sample", None, None), P("space", "sample", None, None), P(), P())
    return jax.shard_map(local, mesh=mesh, in_specs=in_specs, out_specs=out_specs, check_vma=False)
```

```python
import jax
import jax.numpy as jnp
from jax import lax
from jax.sharding import PartitionSpec as P

SIDE = 32


def with_halo(block, sides, width):
    for axis, dim in sides:
        count = lax.axis_size(axis)
        forward = [(i, i + 1) for i in range(count - 1)]
        backward = [(target, source) for source, target in forward]
        low = lax.ppermute(
            lax.slice_in_dim(block, block.shape[dim] - width, None, axis=dim), axis, forward
        )
        high = lax.ppermute(lax.slice_in_dim(block, 0, width, axis=dim), axis, backward)
        block = jnp.concatenate([low, block, high], axis=dim)
    return block


def passed_along(block, axis, distance):
    devices = range(lax.axis_size(axis))
    route = [(i - distance, i) for i in devices if i - distance in devices]
    return lax.ppermute(block, axis, route)


def convolve(inputs, kernel, stride, margins, dilation):
    return lax.conv_general_dilated(
        inputs,
        kernel,
        (stride, stride, stride),
        margins,
        lhs_dilation=(dilation, dilation, dilation),
        dimension_numbers=("DNCHW", "DHWIO", "DNCHW"),
        preferred_element_type=jnp.float32,
    )


def kernel_cube(kernel):
    return kernel.reshape(3, 3, 3, kernel.shape[1], kernel.shape[2])


def reversed_kernel(kernel):
    cube = kernel_cube(kernel)
    return jnp.transpose(cube[::-1, ::-1, ::-1], (0, 1, 2, 4, 3))


def tap_windows(padded, stride, depth_out, rows_out, cols_out):
    if stride == 1:
        phases = padded[None, None]
    else:
        depth, batch, channels, rows, cols = padded.shape
        phases = padded.reshape(depth, batch, channels, rows // 2, 2, cols // 2, 2)
        phases = jnp.transpose(phases, (4, 6, 0, 1, 2, 3, 5))
    windows = []
    for depth_tap in range(3):
        for row_tap in range(3):
            for col_tap in range(3):
                phase = phases[row_tap % stride, col_tap % stride]
                row0, col0 = row_tap // stride, col_tap // stride
                windows.append(
                    lax.slice(
                        phase,
                        (depth_tap, 0, 0, row0, col0),
                        (
                            depth_tap + stride * (depth_out - 1) + 1,
                            phase.shape[1],
                            phase.shape[2],
                            row0 + rows_out,
                            col0 + cols_out,
                        ),
                        (stride, 1, 1, 1, 1),
                    )
                )
    return jnp.stack(windows)


ROUNDS = (
    ("space", 1, 2),
    ("sample", 1, 4),
    ("sample", 4, 2),
    ("space", 8, 4),
    ("space", 2, 4),
)


def group_pairs(count, stride, radix, shift):
    pairs = []
    for i in range(count):
        g = (i // stride) % radix
        pairs.append((i, i + (((g + shift) % radix) - g) * stride))
    return pairs


def picked(g, chunks, shift):
    radix = len(chunks)
    out = chunks[shift % radix]
    for k in range(1, radix):
        out = jnp.where(g == k, chunks[(k + shift) % radix], out)
    return out


def all_sum(parts):
    flat = jnp.concatenate([part.reshape(-1) for part in parts])
    rounds = []
    count = 1
    for axis, stride, radix in ROUNDS:
        if stride * radix <= lax.axis_size(axis):
            rounds.append((axis, stride, radix))
            count *= radix
    total = flat.shape[0]
    value = jnp.pad(flat, (0, -(-total // count) * count - total))
    for axis, stride, radix in rounds:
        size = lax.axis_size(axis)
        g = (lax.axis_index(axis) // stride) % radix
        chunks = jnp.split(value, radix)
        value = picked(g, chunks, 0)
        for shift in range(1, radix):
            sent = picked(g, chunks, shift)
            value = value + lax.ppermute(sent, axis, group_pairs(size, stride, radix, shift))
    for axis, stride, radix in reversed(rounds):
        size = lax.axis_size(axis)
        g = (lax.axis_index(axis) // stride) % radix
        got = [value] + [
            lax.ppermute(value, axis, group_pairs(size, stride, radix, shift))
            for shift in range(1, radix)
        ]
        pieces = []
        for place in range(radix):
            piece = got[(radix - place) % radix]
            for shift in range(radix):
                piece = jnp.where(g == (place + shift) % radix, got[shift], piece)
            pieces.append(piece)
        value = jnp.concatenate(pieces)
    results = []
    offset = 0
    for part in parts:
        results.append(value[offset : offset + part.size].reshape(part.shape))
        offset += part.size
    return results


def column_windows(framed, depth_out):
    depth, batch, channels, side, _ = framed.shape
    plane = side * side
    cells = jnp.transpose(framed.reshape(depth, batch, channels, plane), (2, 1, 0, 3))
    cells = jnp.pad(cells, ((0, 0), (0, 0), (0, 0), (side + 1, side + 1)))
    stacks = []
    for col_tap in range(3):
        windows = []
        for depth_tap in range(3):
            for row_tap in range(3):
                start = (side + 1) + (row_tap - 1) * side + (col_tap - 1)
                windows.append(
                    lax.slice(
                        cells,
                        (0, 0, depth_tap, start),
                        (channels, batch, depth_tap + depth_out, start + plane),
                    )
                )
        stacks.append(jnp.stack(windows))
    return stacks


def edge_masked(values, col_tap, side):
    column = lax.broadcasted_iota(jnp.int32, values.shape, values.ndim - 1) % side
    if col_tap == 0:
        return jnp.where(column == 0, 0, values)
    if col_tap == 2:
        return jnp.where(column == side - 1, 0, values)
    return values


def first_forward(stacks, kernel, side):
    cube = kernel_cube(kernel)
    total = None
    for col_tap in range(3):
        taps = cube[:, :, col_tap].reshape(9, kernel.shape[1], kernel.shape[2])
        part = jnp.einsum("tibzs,tio->zbos", stacks[col_tap], taps, preferred_element_type=jnp.float32)
        part = edge_masked(part, col_tap, side)
        total = part if total is None else total + part
    return total.reshape(total.shape[:3] + (side, side))


def first_weight_grad(stacks, grads):
    depth_out, batch, channels_out, side, _ = grads.shape
    flat_grads = jnp.transpose(grads.reshape(depth_out, batch, channels_out, side * side), (2, 1, 0, 3))
    per_column = []
    for col_tap in range(3):
        masked = edge_masked(flat_grads, col_tap, side)
        per_column.append(
            jnp.einsum(
                "tibzs,obzs->tio",
                stacks[col_tap],
                masked.astype(stacks[col_tap].dtype),
                preferred_element_type=jnp.float32,
            )
        )
    stacked = jnp.stack(per_column, 1)
    return stacked.reshape(27, stacked.shape[2], -1)


def second_weight_grad(hidden, grads, above):
    depth, batch, channels, rows, cols = hidden.shape
    depth_out, rows_out, cols_out = (grads.shape[0], grads.shape[3], grads.shape[4])
    padded = jnp.pad(hidden, ((0, 0), (0, 0), (0, 0), (1, 1), (1, 1)))
    phases = padded.reshape(depth, batch, channels, rows // 2 + 1, 2, cols // 2 + 1, 2)
    phases = jnp.transpose(phases, (4, 6, 0, 1, 2, 3, 5))
    shifted = jnp.concatenate([grads[1:], above[:1]], 0)
    per_depth = []
    for depth_tap, first_plane, tap_grads in ((0, 1, shifted), (1, 0, grads), (2, 1, grads)):
        windows = []
        for row_tap in range(3):
            for col_tap in range(3):
                phase = phases[row_tap % 2, col_tap % 2]
                row0, col0 = row_tap // 2, col_tap // 2
                windows.append(
                    lax.slice(
                        phase,
                        (first_plane, 0, 0, row0, col0),
                        (
                            first_plane + 2 * (depth_out - 1) + 1,
                            batch,
                            channels,
                            row0 + rows_out,
                            col0 + cols_out,
                        ),
                        (2, 1, 1, 1, 1),
                    )
                )
        per_depth.append(
            jnp.einsum(
                "tzbiyx,zboyx->tio",
                jnp.stack(windows),
                tap_grads,
                preferred_element_type=jnp.float32,
            )
        )
    return jnp.stack(per_depth).reshape(27, channels, -1)


def local(volume, out_grads, kernel_one, kernel_two):
    depth, batch, channels_in, plane = volume.shape
    channels_two = kernel_two.shape[2]
    half_side = SIDE // 2
    space_count = lax.axis_size("space")
    sample_count = lax.axis_size("sample")
    scale_one = float(sample_count * batch * space_count * depth * plane) ** (-0.5)
    scale_two = scale_one * 8.0**0.5
    cells = volume.reshape(depth, batch, channels_in, SIDE, SIDE)
    grads_cells = out_grads.reshape(depth // 2, batch, channels_two, half_side, half_side)
    framed = with_halo(cells, (("space", 0),), 1)
    stacks_one = column_windows(framed, depth)
    pre_one = first_forward(stacks_one, kernel_one, SIDE)
    hidden = jax.nn.silu(pre_one).astype(jnp.bfloat16)
    below = passed_along(hidden[-1:], "space", 1)
    stacked = jnp.pad(jnp.concatenate([below, hidden], 0), ((0, 0), (0, 0), (0, 0), (1, 1), (1, 1)))
    windows_two = tap_windows(
        stacked, 2, depth // 2, half_side, half_side
    )
    strided = jnp.einsum(
        "tzbiyx,tio->zboyx", windows_two, kernel_two, preferred_element_type=jnp.float32
    )
    above = passed_along(grads_cells, "space", -1)
    spread = convolve(
        jnp.concatenate([grads_cells, above], 0),
        reversed_kernel(kernel_two),
        1,
        [(1, 0), (1, 2), (1, 2)],
        2,
    )
    hidden_grads = spread.astype(jnp.bfloat16)
    local_two = second_weight_grad(hidden, grads_cells, above) * scale_two
    layer_out = strided.astype(jnp.bfloat16).reshape(depth // 2, batch, channels_two, plane // 4)
    sigma = jax.nn.sigmoid(pre_one)
    pre_grads = (hidden_grads.astype(jnp.float32) * sigma * (1.0 + pre_one * (1.0 - sigma))).astype(
        jnp.bfloat16
    )
    framed_grads = with_halo(pre_grads, (("space", 0),), 1)
    input_grads = convolve(
        framed_grads, reversed_kernel(kernel_one), 1, [(0, 0), (1, 1), (1, 1)], 1
    ).astype(jnp.bfloat16)
    first_grads = first_weight_grad(stacks_one, pre_grads) * scale_one
    first_grads, second_grads = all_sum([first_grads, local_two])
    return (
        layer_out,
        input_grads.reshape(depth, batch, channels_in, plane),
        first_grads,
        second_grads,
    )


def solution(mesh):
    in_specs = (P("space", "sample", None, None), P("space", "sample", None, None), P(), P())
    out_specs = (P("space", "sample", None, None), P("space", "sample", None, None), P(), P())
    return jax.shard_map(local, mesh=mesh, in_specs=in_specs, out_specs=out_specs, check_vma=False)
```

```python
import jax
import jax.numpy as jnp
from jax import lax
from jax.sharding import PartitionSpec as P

SIDE = 32


def with_halo(block, sides, width):
    for axis, dim in sides:
        count = lax.axis_size(axis)
        forward = [(i, i + 1) for i in range(count - 1)]
        backward = [(target, source) for source, target in forward]
        low = lax.ppermute(
            lax.slice_in_dim(block, block.shape[dim] - width, None, axis=dim), axis, forward
        )
        high = lax.ppermute(lax.slice_in_dim(block, 0, width, axis=dim), axis, backward)
        block = jnp.concatenate([low, block, high], axis=dim)
    return block


def passed_along(block, axis, distance):
    devices = range(lax.axis_size(axis))
    route = [(i - distance, i) for i in devices if i - distance in devices]
    return lax.ppermute(block, axis, route)


def convolve(inputs, kernel, stride, margins, dilation):
    return lax.conv_general_dilated(
        inputs,
        kernel,
        (stride, stride, stride),
        margins,
        lhs_dilation=(dilation, dilation, dilation),
        dimension_numbers=("DNCHW", "DHWIO", "DNCHW"),
        preferred_element_type=jnp.float32,
    )


def kernel_cube(kernel):
    return kernel.reshape(3, 3, 3, kernel.shape[1], kernel.shape[2])


def reversed_kernel(kernel):
    cube = kernel_cube(kernel)
    return jnp.transpose(cube[::-1, ::-1, ::-1], (0, 1, 2, 4, 3))


def tap_windows(padded, stride, depth_out, rows_out, cols_out):
    if stride == 1:
        phases = padded[None, None]
    else:
        depth, batch, channels, rows, cols = padded.shape
        phases = padded.reshape(depth, batch, channels, rows // 2, 2, cols // 2, 2)
        phases = jnp.transpose(phases, (4, 6, 0, 1, 2, 3, 5))
    windows = []
    for depth_tap in range(3):
        for row_tap in range(3):
            for col_tap in range(3):
                phase = phases[row_tap % stride, col_tap % stride]
                row0, col0 = row_tap // stride, col_tap // stride
                windows.append(
                    lax.slice(
                        phase,
                        (depth_tap, 0, 0, row0, col0),
                        (
                            depth_tap + stride * (depth_out - 1) + 1,
                            phase.shape[1],
                            phase.shape[2],
                            row0 + rows_out,
                            col0 + cols_out,
                        ),
                        (stride, 1, 1, 1, 1),
                    )
                )
    return jnp.stack(windows)


ROUNDS = (
    ("space", 1, 2),
    ("sample", 4, 2),
    ("sample", 1, 4),
    ("space", 8, 4),
    ("space", 2, 4),
)


def group_pairs(count, stride, radix, shift):
    pairs = []
    for i in range(count):
        g = (i // stride) % radix
        pairs.append((i, i + (((g + shift) % radix) - g) * stride))
    return pairs


def picked(g, chunks, shift):
    radix = len(chunks)
    out = chunks[shift % radix]
    for k in range(1, radix):
        out = jnp.where(g == k, chunks[(k + shift) % radix], out)
    return out


def all_sum(parts):
    flat = jnp.concatenate([part.reshape(-1) for part in parts])
    rounds = []
    count = 1
    for axis, stride, radix in ROUNDS:
        if stride * radix <= lax.axis_size(axis):
            rounds.append((axis, stride, radix))
            count *= radix
    total = flat.shape[0]
    value = jnp.pad(flat, (0, -(-total // count) * count - total))
    for axis, stride, radix in rounds:
        size = lax.axis_size(axis)
        g = (lax.axis_index(axis) // stride) % radix
        chunks = jnp.split(value, radix)
        value = picked(g, chunks, 0)
        for shift in range(1, radix):
            sent = picked(g, chunks, shift)
            value = value + lax.ppermute(sent, axis, group_pairs(size, stride, radix, shift))
    for axis, stride, radix in reversed(rounds):
        size = lax.axis_size(axis)
        g = (lax.axis_index(axis) // stride) % radix
        got = [value] + [
            lax.ppermute(value, axis, group_pairs(size, stride, radix, shift))
            for shift in range(1, radix)
        ]
        pieces = []
        for place in range(radix):
            piece = got[(radix - place) % radix]
            for shift in range(radix):
                piece = jnp.where(g == (place + shift) % radix, got[shift], piece)
            pieces.append(piece)
        value = jnp.concatenate(pieces)
    results = []
    offset = 0
    for part in parts:
        results.append(value[offset : offset + part.size].reshape(part.shape))
        offset += part.size
    return results


def column_windows(framed, depth_out):
    depth, batch, channels, side, _ = framed.shape
    plane = side * side
    cells = jnp.transpose(framed.reshape(depth, batch, channels, plane), (2, 1, 0, 3))
    cells = jnp.pad(cells, ((0, 0), (0, 0), (0, 0), (side + 1, side + 1)))
    stacks = []
    for col_tap in range(3):
        windows = []
        for depth_tap in range(3):
            for row_tap in range(3):
                start = (side + 1) + (row_tap - 1) * side + (col_tap - 1)
                windows.append(
                    lax.slice(
                        cells,
                        (0, 0, depth_tap, start),
                        (channels, batch, depth_tap + depth_out, start + plane),
                    )
                )
        stacks.append(jnp.stack(windows))
    return stacks


def edge_masked(values, col_tap, side):
    column = lax.broadcasted_iota(jnp.int32, values.shape, values.ndim - 1) % side
    if col_tap == 0:
        return jnp.where(column == 0, 0, values)
    if col_tap == 2:
        return jnp.where(column == side - 1, 0, values)
    return values


def first_forward(stacks, kernel, side):
    cube = kernel_cube(kernel)
    total = None
    for col_tap in range(3):
        taps = cube[:, :, col_tap].reshape(9, kernel.shape[1], kernel.shape[2])
        part = jnp.einsum("tibzs,tio->zbos", stacks[col_tap], taps, preferred_element_type=jnp.float32)
        part = edge_masked(part, col_tap, side)
        total = part if total is None else total + part
    return total.reshape(total.shape[:3] + (side, side))


def first_weight_grad(stacks, grads):
    depth_out, batch, channels_out, side, _ = grads.shape
    flat_grads = jnp.transpose(grads.reshape(depth_out, batch, channels_out, side * side), (2, 1, 0, 3))
    per_column = []
    for col_tap in range(3):
        masked = edge_masked(flat_grads, col_tap, side)
        per_column.append(
            jnp.einsum(
                "tibzs,obzs->tio",
                stacks[col_tap],
                masked.astype(stacks[col_tap].dtype),
                preferred_element_type=jnp.float32,
            )
        )
    stacked = jnp.stack(per_column, 1)
    return stacked.reshape(27, stacked.shape[2], -1)


def local(volume, out_grads, kernel_one, kernel_two):
    depth, batch, channels_in, plane = volume.shape
    channels_two = kernel_two.shape[2]
    half_side = SIDE // 2
    space_count = lax.axis_size("space")
    sample_count = lax.axis_size("sample")
    scale_one = float(sample_count * batch * space_count * depth * plane) ** (-0.5)
    scale_two = scale_one * 8.0**0.5
    cells = volume.reshape(depth, batch, channels_in, SIDE, SIDE)
    grads_cells = out_grads.reshape(depth // 2, batch, channels_two, half_side, half_side)
    framed = with_halo(cells, (("space", 0),), 1)
    stacks_one = column_windows(framed, depth)
    pre_one = first_forward(stacks_one, kernel_one, SIDE)
    hidden = jax.nn.silu(pre_one).astype(jnp.bfloat16)
    below = passed_along(hidden[-1:], "space", 1)
    stacked = jnp.pad(jnp.concatenate([below, hidden], 0), ((0, 0), (0, 0), (0, 0), (1, 1), (1, 1)))
    windows_two = tap_windows(
        stacked, 2, depth // 2, half_side, half_side
    )
    strided = jnp.einsum(
        "tzbiyx,tio->zboyx", windows_two, kernel_two, preferred_element_type=jnp.float32
    )
    above = passed_along(grads_cells, "space", -1)
    spread = convolve(
        jnp.concatenate([grads_cells, above], 0),
        reversed_kernel(kernel_two),
        1,
        [(1, 0), (1, 2), (1, 2)],
        2,
    )
    hidden_grads = spread.astype(jnp.bfloat16)
    local_two = jnp.einsum(
        "tzbiyx,zboyx->tio", windows_two, grads_cells, preferred_element_type=jnp.float32
    ) * scale_two
    layer_out = strided.astype(jnp.bfloat16).reshape(depth // 2, batch, channels_two, plane // 4)
    sigma = jax.nn.sigmoid(pre_one)
    pre_grads = (hidden_grads.astype(jnp.float32) * sigma * (1.0 + pre_one * (1.0 - sigma))).astype(
        jnp.bfloat16
    )
    framed_grads = with_halo(pre_grads, (("space", 0),), 1)
    input_grads = convolve(
        framed_grads, reversed_kernel(kernel_one), 1, [(0, 0), (1, 1), (1, 1)], 1
    ).astype(jnp.bfloat16)
    first_grads = first_weight_grad(stacks_one, pre_grads) * scale_one
    first_grads, second_grads = all_sum([first_grads, local_two])
    return (
        layer_out,
        input_grads.reshape(depth, batch, channels_in, plane),
        first_grads,
        second_grads,
    )


def solution(mesh):
    in_specs = (P("space", "sample", None, None), P("space", "sample", None, None), P(), P())
    out_specs = (P("space", "sample", None, None), P("space", "sample", None, None), P(), P())
    return jax.shard_map(local, mesh=mesh, in_specs=in_specs, out_specs=out_specs, check_vma=False)
```

```python
import jax
import jax.numpy as jnp
from jax import lax
from jax.sharding import PartitionSpec as P

SIDE = 32


def with_halo(block, sides, width):
    for axis, dim in sides:
        count = lax.axis_size(axis)
        forward = [(i, i + 1) for i in range(count - 1)]
        backward = [(target, source) for source, target in forward]
        low = lax.ppermute(
            lax.slice_in_dim(block, block.shape[dim] - width, None, axis=dim), axis, forward
        )
        high = lax.ppermute(lax.slice_in_dim(block, 0, width, axis=dim), axis, backward)
        block = jnp.concatenate([low, block, high], axis=dim)
    return block


def passed_along(block, axis, distance):
    devices = range(lax.axis_size(axis))
    route = [(i - distance, i) for i in devices if i - distance in devices]
    return lax.ppermute(block, axis, route)


def convolve(inputs, kernel, stride, margins, dilation):
    return lax.conv_general_dilated(
        inputs,
        kernel,
        (stride, stride, stride),
        margins,
        lhs_dilation=(dilation, dilation, dilation),
        dimension_numbers=("DNCHW", "DHWIO", "DNCHW"),
        preferred_element_type=jnp.float32,
    )


def kernel_cube(kernel):
    return kernel.reshape(3, 3, 3, kernel.shape[1], kernel.shape[2])


def reversed_kernel(kernel):
    cube = kernel_cube(kernel)
    return jnp.transpose(cube[::-1, ::-1, ::-1], (0, 1, 2, 4, 3))


def tap_windows(padded, stride, depth_out, rows_out, cols_out):
    if stride == 1:
        phases = padded[None, None]
    else:
        depth, batch, channels, rows, cols = padded.shape
        phases = padded.reshape(depth, batch, channels, rows // 2, 2, cols // 2, 2)
        phases = jnp.transpose(phases, (4, 6, 0, 1, 2, 3, 5))
    windows = []
    for depth_tap in range(3):
        for row_tap in range(3):
            for col_tap in range(3):
                phase = phases[row_tap % stride, col_tap % stride]
                row0, col0 = row_tap // stride, col_tap // stride
                windows.append(
                    lax.slice(
                        phase,
                        (depth_tap, 0, 0, row0, col0),
                        (
                            depth_tap + stride * (depth_out - 1) + 1,
                            phase.shape[1],
                            phase.shape[2],
                            row0 + rows_out,
                            col0 + cols_out,
                        ),
                        (stride, 1, 1, 1, 1),
                    )
                )
    return jnp.stack(windows)


ROUNDS = (
    ("space", 1, 2),
    ("sample", 1, 4),
    ("sample", 4, 2),
    ("space", 8, 4),
    ("space", 2, 4),
)


def group_pairs(count, stride, radix, shift):
    pairs = []
    for i in range(count):
        g = (i // stride) % radix
        pairs.append((i, i + (((g + shift) % radix) - g) * stride))
    return pairs


def picked(g, chunks, shift):
    radix = len(chunks)
    out = chunks[shift % radix]
    for k in range(1, radix):
        out = jnp.where(g == k, chunks[(k + shift) % radix], out)
    return out


def all_sum(parts):
    flat = jnp.concatenate([part.reshape(-1) for part in parts])
    rounds = []
    count = 1
    for axis, stride, radix in ROUNDS:
        if stride * radix <= lax.axis_size(axis):
            rounds.append((axis, stride, radix))
            count *= radix
    total = flat.shape[0]
    value = jnp.pad(flat, (0, -(-total // count) * count - total))
    for axis, stride, radix in rounds:
        size = lax.axis_size(axis)
        g = (lax.axis_index(axis) // stride) % radix
        chunks = jnp.split(value, radix)
        value = picked(g, chunks, 0)
        for shift in range(1, radix):
            sent = picked(g, chunks, shift)
            value = value + lax.ppermute(sent, axis, group_pairs(size, stride, radix, shift))
    for axis, stride, radix in reversed(rounds):
        size = lax.axis_size(axis)
        g = (lax.axis_index(axis) // stride) % radix
        got = [value] + [
            lax.ppermute(value, axis, group_pairs(size, stride, radix, shift))
            for shift in range(1, radix)
        ]
        pieces = []
        for place in range(radix):
            piece = got[(radix - place) % radix]
            for shift in range(radix):
                piece = jnp.where(g == (place + shift) % radix, got[shift], piece)
            pieces.append(piece)
        value = jnp.concatenate(pieces)
    results = []
    offset = 0
    for part in parts:
        results.append(value[offset : offset + part.size].reshape(part.shape))
        offset += part.size
    return results


def column_windows(framed, depth_out):
    depth, batch, channels, side, _ = framed.shape
    plane = side * side
    cells = jnp.transpose(framed.reshape(depth, batch, channels, plane), (2, 1, 0, 3))
    cells = jnp.pad(cells, ((0, 0), (0, 0), (0, 0), (side + 1, side + 1)))
    stacks = []
    for col_tap in range(3):
        windows = []
        for depth_tap in range(3):
            for row_tap in range(3):
                start = (side + 1) + (row_tap - 1) * side + (col_tap - 1)
                windows.append(
                    lax.slice(
                        cells,
                        (0, 0, depth_tap, start),
                        (channels, batch, depth_tap + depth_out, start + plane),
                    )
                )
        stacks.append(jnp.stack(windows))
    return stacks


def edge_masked(values, col_tap, side):
    column = lax.broadcasted_iota(jnp.int32, values.shape, values.ndim - 1) % side
    if col_tap == 0:
        return jnp.where(column == 0, 0, values)
    if col_tap == 2:
        return jnp.where(column == side - 1, 0, values)
    return values


def first_forward(stacks, kernel, side):
    cube = kernel_cube(kernel)
    total = None
    for col_tap in range(3):
        taps = cube[:, :, col_tap].reshape(9, kernel.shape[1], kernel.shape[2])
        part = jnp.einsum("tibzs,tio->zbos", stacks[col_tap], taps, preferred_element_type=jnp.float32)
        part = edge_masked(part, col_tap, side)
        total = part if total is None else total + part
    return total.reshape(total.shape[:3] + (side, side))


def first_weight_grad(stacks, grads):
    depth_out, batch, channels_out, side, _ = grads.shape
    flat_grads = jnp.transpose(grads.reshape(depth_out, batch, channels_out, side * side), (2, 1, 0, 3))
    per_column = []
    for col_tap in range(3):
        masked = edge_masked(flat_grads, col_tap, side)
        per_column.append(
            jnp.einsum(
                "tibzs,obzs->tio",
                stacks[col_tap],
                masked.astype(stacks[col_tap].dtype),
                preferred_element_type=jnp.float32,
            )
        )
    stacked = jnp.stack(per_column, 1)
    return stacked.reshape(27, stacked.shape[2], -1)


def local(volume, out_grads, kernel_one, kernel_two):
    depth, batch, channels_in, plane = volume.shape
    channels_two = kernel_two.shape[2]
    half_side = SIDE // 2
    space_count = lax.axis_size("space")
    sample_count = lax.axis_size("sample")
    scale_one = float(sample_count * batch * space_count * depth * plane) ** (-0.5)
    scale_two = scale_one * 8.0**0.5
    cells = volume.reshape(depth, batch, channels_in, SIDE, SIDE)
    grads_cells = out_grads.reshape(depth // 2, batch, channels_two, half_side, half_side)
    lower = passed_along(cells[-2:], "space", 1)
    upper = passed_along(cells[:1], "space", -1)
    widened = jnp.concatenate([lower, cells, upper], 0)
    stacks_wide = column_windows(widened, depth + 1)
    stacks_one = [stack[:, :, :, 1:] for stack in stacks_wide]
    pre_wide = first_forward(stacks_wide, kernel_one, SIDE)
    pre_one = pre_wide[1:]
    hidden_wide = jax.nn.silu(pre_wide).astype(jnp.bfloat16)
    hidden = hidden_wide[1:]
    has_below = lax.axis_index("space") > 0
    below = jnp.where(has_below, hidden_wide[:1], jnp.zeros_like(hidden_wide[:1]))
    stacked = jnp.pad(jnp.concatenate([below, hidden], 0), ((0, 0), (0, 0), (0, 0), (1, 1), (1, 1)))
    windows_two = tap_windows(
        stacked, 2, depth // 2, half_side, half_side
    )
    strided = jnp.einsum(
        "tzbiyx,tio->zboyx", windows_two, kernel_two, preferred_element_type=jnp.float32
    )
    above = passed_along(grads_cells, "space", -1)
    spread = convolve(
        jnp.concatenate([grads_cells, above], 0),
        reversed_kernel(kernel_two),
        1,
        [(1, 0), (1, 2), (1, 2)],
        2,
    )
    hidden_grads = spread.astype(jnp.bfloat16)
    local_two = jnp.einsum(
        "tzbiyx,zboyx->tio", windows_two, grads_cells, preferred_element_type=jnp.float32
    ) * scale_two
    layer_out = strided.astype(jnp.bfloat16).reshape(depth // 2, batch, channels_two, plane // 4)
    sigma = jax.nn.sigmoid(pre_one)
    pre_grads = (hidden_grads.astype(jnp.float32) * sigma * (1.0 + pre_one * (1.0 - sigma))).astype(
        jnp.bfloat16
    )
    framed_grads = with_halo(pre_grads, (("space", 0),), 1)
    input_grads = convolve(
        framed_grads, reversed_kernel(kernel_one), 1, [(0, 0), (1, 1), (1, 1)], 1
    ).astype(jnp.bfloat16)
    first_grads = first_weight_grad(stacks_one, pre_grads) * scale_one
    first_grads, second_grads = all_sum([first_grads, local_two])
    return (
        layer_out,
        input_grads.reshape(depth, batch, channels_in, plane),
        first_grads,
        second_grads,
    )


def solution(mesh):
    in_specs = (P("space", "sample", None, None), P("space", "sample", None, None), P(), P())
    out_specs = (P("space", "sample", None, None), P("space", "sample", None, None), P(), P())
    return jax.shard_map(local, mesh=mesh, in_specs=in_specs, out_specs=out_specs, check_vma=False)
```

```python
import jax
import jax.numpy as jnp
from jax import lax
from jax.sharding import PartitionSpec as P

SIDE = 32


def with_halo(block, sides, width):
    for axis, dim in sides:
        count = lax.axis_size(axis)
        forward = [(i, i + 1) for i in range(count - 1)]
        backward = [(target, source) for source, target in forward]
        low = lax.ppermute(
            lax.slice_in_dim(block, block.shape[dim] - width, None, axis=dim), axis, forward
        )
        high = lax.ppermute(lax.slice_in_dim(block, 0, width, axis=dim), axis, backward)
        block = jnp.concatenate([low, block, high], axis=dim)
    return block


def passed_along(block, axis, distance):
    devices = range(lax.axis_size(axis))
    route = [(i - distance, i) for i in devices if i - distance in devices]
    return lax.ppermute(block, axis, route)


def convolve(inputs, kernel, stride, margins, dilation):
    return lax.conv_general_dilated(
        inputs,
        kernel,
        (stride, stride, stride),
        margins,
        lhs_dilation=(dilation, dilation, dilation),
        dimension_numbers=("DNCHW", "DHWIO", "DNCHW"),
        preferred_element_type=jnp.float32,
    )


def kernel_cube(kernel):
    return kernel.reshape(3, 3, 3, kernel.shape[1], kernel.shape[2])


def reversed_kernel(kernel):
    cube = kernel_cube(kernel)
    return jnp.transpose(cube[::-1, ::-1, ::-1], (0, 1, 2, 4, 3))


def tap_windows(padded, stride, depth_out, rows_out, cols_out):
    if stride == 1:
        phases = padded[None, None]
    else:
        depth, batch, channels, rows, cols = padded.shape
        phases = padded.reshape(depth, batch, channels, rows // 2, 2, cols // 2, 2)
        phases = jnp.transpose(phases, (4, 6, 0, 1, 2, 3, 5))
    windows = []
    for depth_tap in range(3):
        for row_tap in range(3):
            for col_tap in range(3):
                phase = phases[row_tap % stride, col_tap % stride]
                row0, col0 = row_tap // stride, col_tap // stride
                windows.append(
                    lax.slice(
                        phase,
                        (depth_tap, 0, 0, row0, col0),
                        (
                            depth_tap + stride * (depth_out - 1) + 1,
                            phase.shape[1],
                            phase.shape[2],
                            row0 + rows_out,
                            col0 + cols_out,
                        ),
                        (stride, 1, 1, 1, 1),
                    )
                )
    return jnp.stack(windows)


ROUNDS = (
    ("space", 1, 2),
    ("sample", 1, 4),
    ("sample", 4, 2),
    ("space", 8, 4),
    ("space", 2, 4),
)


def group_pairs(count, stride, radix, shift):
    pairs = []
    for i in range(count):
        g = (i // stride) % radix
        pairs.append((i, i + (((g + shift) % radix) - g) * stride))
    return pairs


def picked(g, chunks, shift):
    radix = len(chunks)
    out = chunks[shift % radix]
    for k in range(1, radix):
        out = jnp.where(g == k, chunks[(k + shift) % radix], out)
    return out


def all_sum(parts):
    flat = jnp.concatenate([part.reshape(-1) for part in parts])
    rounds = []
    count = 1
    for axis, stride, radix in ROUNDS:
        if stride * radix <= lax.axis_size(axis):
            rounds.append((axis, stride, radix))
            count *= radix
    total = flat.shape[0]
    value = jnp.pad(flat, (0, -(-total // count) * count - total))
    for axis, stride, radix in rounds:
        size = lax.axis_size(axis)
        g = (lax.axis_index(axis) // stride) % radix
        chunks = jnp.split(value, radix)
        value = picked(g, chunks, 0)
        for shift in range(1, radix):
            sent = picked(g, chunks, shift)
            value = value + lax.ppermute(sent, axis, group_pairs(size, stride, radix, shift))
    for axis, stride, radix in reversed(rounds):
        size = lax.axis_size(axis)
        g = (lax.axis_index(axis) // stride) % radix
        got = [value] + [
            lax.ppermute(value, axis, group_pairs(size, stride, radix, shift))
            for shift in range(1, radix)
        ]
        pieces = []
        for place in range(radix):
            piece = got[(radix - place) % radix]
            for shift in range(radix):
                piece = jnp.where(g == (place + shift) % radix, got[shift], piece)
            pieces.append(piece)
        value = jnp.concatenate(pieces)
    results = []
    offset = 0
    for part in parts:
        results.append(value[offset : offset + part.size].reshape(part.shape))
        offset += part.size
    return results


def column_windows(framed, depth_out):
    depth, batch, channels, side, _ = framed.shape
    plane = side * side
    cells = jnp.transpose(framed.reshape(depth, batch, channels, plane), (2, 1, 0, 3))
    cells = jnp.pad(cells, ((0, 0), (0, 0), (0, 0), (side + 1, side + 1)))
    stacks = []
    for col_tap in range(3):
        windows = []
        for depth_tap in range(3):
            for row_tap in range(3):
                start = (side + 1) + (row_tap - 1) * side + (col_tap - 1)
                windows.append(
                    lax.slice(
                        cells,
                        (0, 0, depth_tap, start),
                        (channels, batch, depth_tap + depth_out, start + plane),
                    )
                )
        stacks.append(jnp.stack(windows))
    return stacks


def edge_masked(values, col_tap, side):
    column = lax.broadcasted_iota(jnp.int32, values.shape, values.ndim - 1) % side
    if col_tap == 0:
        return jnp.where(column == 0, 0, values)
    if col_tap == 2:
        return jnp.where(column == side - 1, 0, values)
    return values


def first_forward(stacks, kernel, side):
    cube = kernel_cube(kernel)
    total = None
    for col_tap in range(3):
        taps = cube[:, :, col_tap].reshape(9, kernel.shape[1], kernel.shape[2])
        part = jnp.einsum("tibzs,tio->zbos", stacks[col_tap], taps, preferred_element_type=jnp.float32)
        part = edge_masked(part, col_tap, side)
        total = part if total is None else total + part
    return total.reshape(total.shape[:3] + (side, side))


def first_weight_grad(stacks, grads):
    depth_out, batch, channels_out, side, _ = grads.shape
    flat_grads = jnp.transpose(grads.reshape(depth_out, batch, channels_out, side * side), (2, 1, 0, 3))
    per_column = []
    for col_tap in range(3):
        masked = edge_masked(flat_grads, col_tap, side)
        per_column.append(
            jnp.einsum(
                "tibzs,obzs->tio",
                stacks[col_tap],
                masked.astype(stacks[col_tap].dtype),
                preferred_element_type=jnp.float32,
            )
        )
    stacked = jnp.stack(per_column, 1)
    return stacked.reshape(27, stacked.shape[2], -1)


def local(volume, out_grads, kernel_one, kernel_two):
    depth, batch, channels_in, plane = volume.shape
    channels_two = kernel_two.shape[2]
    half_side = SIDE // 2
    space_count = lax.axis_size("space")
    sample_count = lax.axis_size("sample")
    scale_one = float(sample_count * batch * space_count * depth * plane) ** (-0.5)
    scale_two = scale_one * 8.0**0.5
    cells = volume.reshape(depth, batch, channels_in, SIDE, SIDE)
    grads_cells = out_grads.reshape(depth // 2, batch, channels_two, half_side, half_side)
    framed = with_halo(cells, (("space", 0),), 1)
    stacks_one = column_windows(framed, depth)
    pre_one = first_forward(stacks_one, kernel_one, SIDE)
    hidden = jax.nn.silu(pre_one).astype(jnp.bfloat16)
    below = passed_along(hidden[-1:], "space", 1)
    stacked = jnp.pad(jnp.concatenate([below, hidden], 0), ((0, 0), (0, 0), (0, 0), (1, 1), (1, 1)))
    windows_two = tap_windows(
        stacked, 2, depth // 2, half_side, half_side
    )
    strided = jnp.einsum(
        "tzbiyx,tio->zboyx", windows_two, kernel_two, preferred_element_type=jnp.float32
    )
    above = passed_along(grads_cells, "space", -1)
    spread = convolve(
        jnp.concatenate([grads_cells, above], 0),
        reversed_kernel(kernel_two),
        1,
        [(1, 0), (1, 2), (1, 2)],
        2,
    )
    hidden_grads = spread.astype(jnp.bfloat16)
    local_two = jnp.einsum(
        "tzbiyx,zboyx->tio", windows_two, grads_cells, preferred_element_type=jnp.float32
    ) * scale_two
    layer_out = strided.astype(jnp.bfloat16).reshape(depth // 2, batch, channels_two, plane // 4)
    sigma = jax.nn.sigmoid(pre_one)
    pre_grads = (hidden_grads.astype(jnp.float32) * sigma * (1.0 + pre_one * (1.0 - sigma))).astype(
        jnp.bfloat16
    )
    framed_grads = with_halo(pre_grads, (("space", 0),), 1)
    first_grads = first_weight_grad(stacks_one, pre_grads) * scale_one
    first_grads, local_two, framed_grads = lax.optimization_barrier(
        (first_grads, local_two, framed_grads)
    )
    input_grads = convolve(
        framed_grads, reversed_kernel(kernel_one), 1, [(0, 0), (1, 1), (1, 1)], 1
    ).astype(jnp.bfloat16)
    first_grads, second_grads = all_sum([first_grads, local_two])
    return (
        layer_out,
        input_grads.reshape(depth, batch, channels_in, plane),
        first_grads,
        second_grads,
    )


def solution(mesh):
    in_specs = (P("space", "sample", None, None), P("space", "sample", None, None), P(), P())
    out_specs = (P("space", "sample", None, None), P("space", "sample", None, None), P(), P())
    return jax.shard_map(local, mesh=mesh, in_specs=in_specs, out_specs=out_specs, check_vma=False)
```

```python
import jax
import jax.numpy as jnp
from jax import lax
from jax.sharding import PartitionSpec as P

SIDE = 32


def with_halo(block, sides, width):
    for axis, dim in sides:
        count = lax.axis_size(axis)
        forward = [(i, i + 1) for i in range(count - 1)]
        backward = [(target, source) for source, target in forward]
        low = lax.ppermute(
            lax.slice_in_dim(block, block.shape[dim] - width, None, axis=dim), axis, forward
        )
        high = lax.ppermute(lax.slice_in_dim(block, 0, width, axis=dim), axis, backward)
        block = jnp.concatenate([low, block, high], axis=dim)
    return block


def passed_along(block, axis, distance):
    devices = range(lax.axis_size(axis))
    route = [(i - distance, i) for i in devices if i - distance in devices]
    return lax.ppermute(block, axis, route)


def convolve(inputs, kernel, stride, margins, dilation):
    return lax.conv_general_dilated(
        inputs,
        kernel,
        (stride, stride, stride),
        margins,
        lhs_dilation=(dilation, dilation, dilation),
        dimension_numbers=("DNCHW", "DHWIO", "DNCHW"),
        preferred_element_type=jnp.float32,
    )


def kernel_cube(kernel):
    return kernel.reshape(3, 3, 3, kernel.shape[1], kernel.shape[2])


def reversed_kernel(kernel):
    cube = kernel_cube(kernel)
    return jnp.transpose(cube[::-1, ::-1, ::-1], (0, 1, 2, 4, 3))


def tap_windows(padded, stride, depth_out, rows_out, cols_out):
    if stride == 1:
        phases = padded[None, None]
    else:
        depth, batch, channels, rows, cols = padded.shape
        phases = padded.reshape(depth, batch, channels, rows // 2, 2, cols // 2, 2)
        phases = jnp.transpose(phases, (4, 6, 0, 1, 2, 3, 5))
    windows = []
    for depth_tap in range(3):
        for row_tap in range(3):
            for col_tap in range(3):
                phase = phases[row_tap % stride, col_tap % stride]
                row0, col0 = row_tap // stride, col_tap // stride
                windows.append(
                    lax.slice(
                        phase,
                        (depth_tap, 0, 0, row0, col0),
                        (
                            depth_tap + stride * (depth_out - 1) + 1,
                            phase.shape[1],
                            phase.shape[2],
                            row0 + rows_out,
                            col0 + cols_out,
                        ),
                        (stride, 1, 1, 1, 1),
                    )
                )
    return jnp.stack(windows)


ROUNDS = (
    ("space", 1, 2),
    ("sample", 1, 4),
    ("sample", 4, 2),
    ("space", 2, 4),
    ("space", 8, 4),
)


def group_pairs(count, stride, radix, shift):
    pairs = []
    for i in range(count):
        g = (i // stride) % radix
        pairs.append((i, i + (((g + shift) % radix) - g) * stride))
    return pairs


def picked(g, chunks, shift):
    radix = len(chunks)
    out = chunks[shift % radix]
    for k in range(1, radix):
        out = jnp.where(g == k, chunks[(k + shift) % radix], out)
    return out


def all_sum(parts):
    flat = jnp.concatenate([part.reshape(-1) for part in parts])
    rounds = []
    count = 1
    for axis, stride, radix in ROUNDS:
        if stride * radix <= lax.axis_size(axis):
            rounds.append((axis, stride, radix))
            count *= radix
    total = flat.shape[0]
    value = jnp.pad(flat, (0, -(-total // count) * count - total))
    for axis, stride, radix in rounds:
        size = lax.axis_size(axis)
        g = (lax.axis_index(axis) // stride) % radix
        chunks = jnp.split(value, radix)
        value = picked(g, chunks, 0)
        for shift in range(1, radix):
            sent = picked(g, chunks, shift)
            value = value + lax.ppermute(sent, axis, group_pairs(size, stride, radix, shift))
    for axis, stride, radix in reversed(rounds):
        size = lax.axis_size(axis)
        g = (lax.axis_index(axis) // stride) % radix
        got = [value] + [
            lax.ppermute(value, axis, group_pairs(size, stride, radix, shift))
            for shift in range(1, radix)
        ]
        pieces = []
        for place in range(radix):
            piece = got[(radix - place) % radix]
            for shift in range(radix):
                piece = jnp.where(g == (place + shift) % radix, got[shift], piece)
            pieces.append(piece)
        value = jnp.concatenate(pieces)
    results = []
    offset = 0
    for part in parts:
        results.append(value[offset : offset + part.size].reshape(part.shape))
        offset += part.size
    return results


def column_windows(framed, depth_out):
    depth, batch, channels, side, _ = framed.shape
    plane = side * side
    cells = jnp.transpose(framed.reshape(depth, batch, channels, plane), (2, 1, 0, 3))
    cells = jnp.pad(cells, ((0, 0), (0, 0), (0, 0), (side + 1, side + 1)))
    stacks = []
    for col_tap in range(3):
        windows = []
        for depth_tap in range(3):
            for row_tap in range(3):
                start = (side + 1) + (row_tap - 1) * side + (col_tap - 1)
                windows.append(
                    lax.slice(
                        cells,
                        (0, 0, depth_tap, start),
                        (channels, batch, depth_tap + depth_out, start + plane),
                    )
                )
        stacks.append(jnp.stack(windows))
    return stacks


def edge_masked(values, col_tap, side):
    column = lax.broadcasted_iota(jnp.int32, values.shape, values.ndim - 1) % side
    if col_tap == 0:
        return jnp.where(column == 0, 0, values)
    if col_tap == 2:
        return jnp.where(column == side - 1, 0, values)
    return values


def first_forward(stacks, kernel, side):
    cube = kernel_cube(kernel)
    total = None
    for col_tap in range(3):
        taps = cube[:, :, col_tap].reshape(9, kernel.shape[1], kernel.shape[2])
        part = jnp.einsum("tibzs,tio->zbos", stacks[col_tap], taps, preferred_element_type=jnp.float32)
        part = edge_masked(part, col_tap, side)
        total = part if total is None else total + part
    return total.reshape(total.shape[:3] + (side, side))


def first_weight_grad(stacks, grads):
    depth_out, batch, channels_out, side, _ = grads.shape
    flat_grads = jnp.transpose(grads.reshape(depth_out, batch, channels_out, side * side), (2, 1, 0, 3))
    per_column = []
    for col_tap in range(3):
        masked = edge_masked(flat_grads, col_tap, side)
        per_column.append(
            jnp.einsum(
                "tibzs,obzs->tio",
                stacks[col_tap],
                masked.astype(stacks[col_tap].dtype),
                preferred_element_type=jnp.float32,
            )
        )
    stacked = jnp.stack(per_column, 1)
    return stacked.reshape(27, stacked.shape[2], -1)


def local(volume, out_grads, kernel_one, kernel_two):
    depth, batch, channels_in, plane = volume.shape
    channels_two = kernel_two.shape[2]
    half_side = SIDE // 2
    space_count = lax.axis_size("space")
    sample_count = lax.axis_size("sample")
    scale_one = float(sample_count * batch * space_count * depth * plane) ** (-0.5)
    scale_two = scale_one * 8.0**0.5
    cells = volume.reshape(depth, batch, channels_in, SIDE, SIDE)
    grads_cells = out_grads.reshape(depth // 2, batch, channels_two, half_side, half_side)
    framed = with_halo(cells, (("space", 0),), 1)
    stacks_one = column_windows(framed, depth)
    pre_one = first_forward(stacks_one, kernel_one, SIDE)
    hidden = jax.nn.silu(pre_one).astype(jnp.bfloat16)
    below = passed_along(hidden[-1:], "space", 1)
    stacked = jnp.pad(jnp.concatenate([below, hidden], 0), ((0, 0), (0, 0), (0, 0), (1, 1), (1, 1)))
    windows_two = tap_windows(
        stacked, 2, depth // 2, half_side, half_side
    )
    strided = jnp.einsum(
        "tzbiyx,tio->zboyx", windows_two, kernel_two, preferred_element_type=jnp.float32
    )
    above = passed_along(grads_cells, "space", -1)
    spread = convolve(
        jnp.concatenate([grads_cells, above], 0),
        reversed_kernel(kernel_two),
        1,
        [(1, 0), (1, 2), (1, 2)],
        2,
    )
    hidden_grads = spread.astype(jnp.bfloat16)
    local_two = jnp.einsum(
        "tzbiyx,zboyx->tio", windows_two, grads_cells, preferred_element_type=jnp.float32
    ) * scale_two
    layer_out = strided.astype(jnp.bfloat16).reshape(depth // 2, batch, channels_two, plane // 4)
    sigma = jax.nn.sigmoid(pre_one)
    pre_grads = (hidden_grads.astype(jnp.float32) * sigma * (1.0 + pre_one * (1.0 - sigma))).astype(
        jnp.bfloat16
    )
    framed_grads = with_halo(pre_grads, (("space", 0),), 1)
    input_grads = convolve(
        framed_grads, reversed_kernel(kernel_one), 1, [(0, 0), (1, 1), (1, 1)], 1
    ).astype(jnp.bfloat16)
    first_grads = first_weight_grad(stacks_one, pre_grads) * scale_one
    first_grads, second_grads = all_sum([first_grads, local_two])
    return (
        layer_out,
        input_grads.reshape(depth, batch, channels_in, plane),
        first_grads,
        second_grads,
    )


def solution(mesh):
    in_specs = (P("space", "sample", None, None), P("space", "sample", None, None), P(), P())
    out_specs = (P("space", "sample", None, None), P("space", "sample", None, None), P(), P())
    return jax.shard_map(local, mesh=mesh, in_specs=in_specs, out_specs=out_specs, check_vma=False)
```
